128 devices in a mesh: lat: 8 (over y, core), lon: 16 (over x, z).
Axes of the slice: x: 4, y: 4, z: 4, core: 2. Of those that a mesh axis runs over, the one named last changes fastest.
Arguments:
- latent: bfloat16 [128, 1536, 256], P('lat', 'lon'), may hold values from -6 to 6
- ocean_mask: int32 [128, 1536], P('lat', 'lon'), may hold values from 0 to 1, as said below
- depth_kernel: bfloat16 [7, 7, 256], replicated, may hold values from -0.875 to 0.875
- expand_weight: bfloat16 [256, 1024], replicated, may hold values from -0.375 to 0.375
- reduce_weight: bfloat16 [1024, 256], replicated, may hold values from -0.1875 to 0.1875
- decode_weight: bfloat16 [256, 304], replicated, may hold values from -0.375 to 0.375
- column_in: bfloat16 [304, 1024], replicated, may hold values from -0.3125 to 0.3125
- column_out: bfloat16 [1024, 304], replicated, may hold values from -0.1875 to 0.1875
- state_cot: bfloat16 [128, 1536, 304], P('lat', 'lon'), may hold values from -6 to 6
Outputs:
- state: bfloat16 [128, 1536, 304], P('lat', 'lon')
- grad_latent: bfloat16 [128, 1536, 256], P('lat', 'lon')
- grad_kernel: float32 [7, 7, 256], P(None, None, ('lat', 'lon'))
- grad_expand: float32 [256, 1024], P(None, ('lat', 'lon'))
- grad_reduce: float32 [1024, 256], P(('lat', 'lon'))
- grad_decode: float32 [256, 304], P(('lat', 'lon'))
- grad_column_in: float32 [304, 1024], P(None, ('lat', 'lon'))
- grad_column_out: float32 [1024, 304], P(('lat', 'lon'))
The draws below stay inside these ranges and needn't reach their ends.
Inputs may be any that keep to these rules, and one draw needn't show every extreme that they name: `ocean_mask`: exactly 73728 cells are ocean (1), the rest land (0); at least one device's tile is all ocean.
All inputs are finite; a program needn't handle non-finite values.
Results may differ from the reference program's by a relative error of at most 0.008.
Values may be sent and summed in bfloat16 or wider, within the bound.
No kernel may reach another device: no remote copies, remote signals or barrier semaphores. Data moves between devices by JAX's collectives and lax.ppermute only.
A program may use at most 128 MiB of HBM per device.

```python
import math
import jax
import jax.numpy as jnp
from jax import lax

C = 256
EXPAND = 1024
COLVALS = 304
COLHID = 1024
KERNEL = 7
HL = 16
WL = 96
NLAT = 128
NLON = 1536
OCEAN = 73728


def draw_ocean_mask(key, part):
    tile_key, full_key, cell_key, order_key = jax.random.split(key, 4)
    tiles_lat = NLAT // HL
    tiles_lon = NLON // WL
    tile_total = tiles_lat * tiles_lon
    levels = jax.random.randint(tile_key, (tile_total,), 0, 6)
    full_tile = jax.random.randint(full_key, (), 0, tile_total)
    levels = jnp.where(jnp.arange(tile_total) == full_tile, -4, levels)
    lat_ids = jnp.arange(NLAT) // HL
    lon_ids = jnp.arange(NLON) // WL
    tile_ids = (lat_ids[:, None] * tiles_lon + lon_ids[None, :]).reshape(-1)
    scores = levels[tile_ids] + jax.random.randint(cell_key, (NLAT * NLON,), 0, 4)
    shuffled = jax.random.permutation(order_key, NLAT * NLON)
    ordering = shuffled[jnp.argsort(scores[shuffled], stable=True)]
    rank_of = jnp.zeros((NLAT * NLON,), jnp.int32).at[ordering].set(jnp.arange(NLAT * NLON, dtype=jnp.int32))
    return (rank_of < OCEAN).astype(jnp.int32).reshape(NLAT, NLON)


def block_levels(stream_key, shape, pieces, smallest, high):
    level = 1.0
    for axis_at, parts in pieces:
        heights = jax.random.uniform(jax.random.fold_in(jax.random.fold_in(stream_key, 6), axis_at), (parts,), jnp.float32, smallest / len(pieces), high / len(pieces))
        level = level * jnp.repeat(jnp.exp(heights), shape[axis_at] // parts).reshape((-1,) + (1,) * (len(shape) - 1 - axis_at))
    return level


def bell_draw(rng, shape, scale, bound, cuts=(), held_as=jnp.bfloat16):
    level = block_levels(rng, shape, cuts, -0.22, 0.18) if cuts else 1.0
    entries = jax.random.normal(rng, shape, jnp.float32) * scale * level
    return jnp.minimum(jnp.maximum(entries, -bound), bound).astype(held_as)


def setup_inputs(seed: int = 0) -> dict:
    splits = jax.random.split(jax.random.key(seed), 10)
    return {
        "latent": bell_draw(splits[0], (NLAT, NLON, C), 1.0, 6.0, ((0, 8), (1, 16))),
        "ocean_mask": draw_ocean_mask(jax.random.fold_in(splits[9], 71), 0),
        "depth_kernel": bell_draw(splits[2], (KERNEL, KERNEL, C), (KERNEL * KERNEL) ** -0.5, 0.875),
        "expand_weight": bell_draw(splits[3], (C, EXPAND), C ** -0.5, 0.375),
        "reduce_weight": bell_draw(splits[4], (EXPAND, C), EXPAND ** -0.5, 0.1875),
        "decode_weight": bell_draw(splits[5], (C, COLVALS), C ** -0.5, 0.375),
        "column_in": bell_draw(splits[6], (COLVALS, COLHID), COLVALS ** -0.5, 0.3125),
        "column_out": bell_draw(splits[7], (COLHID, COLVALS), COLHID ** -0.5, 0.1875),
        "state_cot": bell_draw(splits[8], (NLAT, NLON, COLVALS), 1.0, 6.0, ((0, 8), (1, 16))),
    }


EPSILON = 1e-06

def gelu_fn(values_in):
    return jax.nn.gelu(values_in, approximate=True)

def gelu_back(pre_act, upstream):
    return jax.vjp(gelu_fn, pre_act)[1](upstream)[0]

def pad_grid(grid_field):
    radius_cells = KERNEL // 2
    wrapped = jnp.concatenate([grid_field[:, -radius_cells:], grid_field, grid_field[:, :radius_cells]], axis=1)
    return jnp.pad(wrapped, ((radius_cells, radius_cells), (0, 0), (0, 0)))

def depthwise(padded, kernel, row_count, col_count):
    summed = jnp.zeros((row_count, col_count, padded.shape[2]), jnp.float32)
    for row_off in range(kernel.shape[0]):
        for col_off in range(kernel.shape[1]):
            window = padded[row_off:row_off + row_count, col_off:col_off + col_count].astype(jnp.float32)
            summed = summed + kernel[row_off, col_off].astype(jnp.float32) * window
    return summed

def back_conv(wide_grad, kernel, row_count, col_count):
    kernel_span = kernel.shape[0] - 1
    summed = jnp.zeros((row_count, col_count, wide_grad.shape[2]), jnp.float32)
    for row_off in range(kernel.shape[0]):
        for col_off in range(kernel.shape[1]):
            low_row = kernel_span - row_off
            low_col = kernel_span - col_off
            window = wide_grad[low_row:low_row + row_count, low_col:low_col + col_count].astype(jnp.float32)
            summed = summed + kernel[row_off, col_off].astype(jnp.float32) * window
    return summed

def kernel_terms(wide_field, grad_field, kernel_size):
    row_count = grad_field.shape[0]
    col_count = grad_field.shape[1]
    terms_list = []
    for row_off in range(kernel_size):
        for col_off in range(kernel_size):
            window = wide_field[row_off:row_off + row_count, col_off:col_off + col_count].astype(jnp.float32)
            terms_list.append(lax.optimization_barrier(jnp.sum(grad_field * window, axis=(0, 1))))
    return jnp.stack(terms_list).reshape(kernel_size, kernel_size, grad_field.shape[2])

def reference(latent, ocean_mask, depth_kernel, expand_weight, reduce_weight, decode_weight, column_in, column_out, state_cot):
    ocean = ocean_mask.astype(latent.dtype)
    masked = latent * ocean[:, :, None]
    padded = pad_grid(masked)
    convolved = depthwise(padded, depth_kernel, NLAT, NLON)
    block_total = NLAT // HL
    block_cells = HL * NLON
    conv_blocks = convolved.reshape(block_total, block_cells, C)
    masked_blocks = masked.reshape(block_total, block_cells, C)
    ocean_blocks = ocean_mask.reshape(block_total, block_cells)
    cot_blocks = state_cot.reshape(block_total, block_cells, COLVALS)

    def block_step(carry, block_data):
        conv_rows, masked_rows, ocean_rows, cot_rows = block_data
        row_mean = lax.optimization_barrier(jnp.mean(conv_rows, axis=1, keepdims=True))
        centred = conv_rows - row_mean
        inverse_scale = lax.rsqrt(lax.optimization_barrier(jnp.mean(centred * centred, axis=1, keepdims=True)) + EPSILON)
        unit_rows = centred * inverse_scale
        normed = unit_rows.astype(jnp.bfloat16)
        expand_pre = jnp.dot(normed, expand_weight, preferred_element_type=jnp.float32)
        hidden = gelu_fn(expand_pre).astype(jnp.bfloat16)
        feature = (masked_rows.astype(jnp.float32) + jnp.dot(hidden, reduce_weight, preferred_element_type=jnp.float32)).astype(jnp.bfloat16)
        column = jnp.dot(feature, decode_weight, preferred_element_type=jnp.float32).astype(jnp.bfloat16)
        column_pre = jnp.dot(column, column_in, preferred_element_type=jnp.float32)
        inner = gelu_fn(column_pre).astype(jnp.bfloat16)
        ocean_col = ocean_rows.astype(jnp.float32)[:, None]
        state_rows = (ocean_col * (column.astype(jnp.float32) + jnp.dot(inner, column_out, preferred_element_type=jnp.float32))).astype(jnp.bfloat16)
        target = (cot_rows.astype(jnp.float32) * ocean_col).astype(jnp.bfloat16)
        inner_back = jnp.dot(target, column_out.T, preferred_element_type=jnp.float32)
        column_pre_grad = gelu_back(column_pre, inner_back).astype(jnp.bfloat16)
        column_grad = (target.astype(jnp.float32) + jnp.dot(column_pre_grad, column_in.T, preferred_element_type=jnp.float32)).astype(jnp.bfloat16)
        feature_back = jnp.dot(column_grad, decode_weight.T, preferred_element_type=jnp.float32)
        feature_grad = feature_back.astype(jnp.bfloat16)
        hidden_back = jnp.dot(feature_grad, reduce_weight.T, preferred_element_type=jnp.float32)
        expand_grad = gelu_back(expand_pre, hidden_back).astype(jnp.bfloat16)
        normed_back = jnp.dot(expand_grad, expand_weight.T, preferred_element_type=jnp.float32)
        conv_grad = (inverse_scale * (normed_back - lax.optimization_barrier(jnp.mean(normed_back, axis=1, keepdims=True)) - unit_rows * lax.optimization_barrier(jnp.mean(normed_back * unit_rows, axis=1, keepdims=True)))).astype(jnp.bfloat16)
        grad_expand, grad_reduce, grad_decode, grad_cin, grad_cout = carry
        grad_expand = grad_expand + jnp.dot(normed.T, expand_grad, preferred_element_type=jnp.float32)
        grad_reduce = grad_reduce + jnp.dot(hidden.T, feature_grad, preferred_element_type=jnp.float32)
        grad_decode = grad_decode + jnp.dot(feature.T, column_grad, preferred_element_type=jnp.float32)
        grad_cin = grad_cin + jnp.dot(column.T, column_pre_grad, preferred_element_type=jnp.float32)
        grad_cout = grad_cout + jnp.dot(inner.T, target, preferred_element_type=jnp.float32)
        return ((grad_expand, grad_reduce, grad_decode, grad_cin, grad_cout), (state_rows, conv_grad, feature_back))
    start_grads = (jnp.zeros((C, EXPAND), jnp.float32), jnp.zeros((EXPAND, C), jnp.float32), jnp.zeros((C, COLVALS), jnp.float32), jnp.zeros((COLVALS, COLHID), jnp.float32), jnp.zeros((COLHID, COLVALS), jnp.float32))
    final_grads, block_outs = lax.scan(block_step, start_grads, (conv_blocks, masked_blocks, ocean_blocks, cot_blocks))
    state_blocks, conv_grad_blocks, feature_blocks = block_outs
    state = state_blocks.reshape(NLAT, NLON, COLVALS)
    conv_grad = conv_grad_blocks.reshape(NLAT, NLON, C)
    feature_back = feature_blocks.reshape(NLAT, NLON, C)
    wide_grad = pad_grid(conv_grad)
    grad_kernel = kernel_terms(padded, conv_grad.astype(jnp.float32), KERNEL)
    back_terms = back_conv(wide_grad, depth_kernel, NLAT, NLON)
    grad_latent = (ocean_mask.astype(jnp.float32)[:, :, None] * (feature_back + back_terms)).astype(jnp.bfloat16)
    grad_scale = 1.0 / math.sqrt(NLAT * NLON)
    grad_expand, grad_reduce, grad_decode, grad_cin, grad_cout = final_grads
    return (state, grad_latent, grad_kernel * grad_scale, grad_expand * grad_scale, grad_reduce * grad_scale, grad_decode * grad_scale, grad_cin * grad_scale, grad_cout * grad_scale)
```

```python
import math

import jax
import jax.numpy as jnp
from jax import lax
from jax.sharding import PartitionSpec as P

KERNEL = 7


EPSILON = 1e-06


def extended(cells, sides, width):
    for axis, dim in sides:
        count = lax.axis_size(axis)
        head = lax.slice_in_dim(cells, 0, width, axis=dim)
        tail = lax.slice_in_dim(cells, cells.shape[dim] - width, cells.shape[dim], axis=dim)
        cells = jnp.concatenate(
            [
                lax.ppermute(tail, axis, [(i, (i + 1) % count) for i in range(count)]),
                cells,
                lax.ppermute(head, axis, [((i + 1) % count, i) for i in range(count)]),
            ],
            axis=dim,
        )
    return cells


def gelu_fn(values_in):
    return jax.nn.gelu(values_in, approximate=True)


def gelu_back(pre_act, upstream):
    return jax.vjp(gelu_fn, pre_act)[1](upstream)[0]


def rim_field(tile_field):
    radius_cells = KERNEL // 2
    widened = extended(tile_field, (("lat", 0), ("lon", 1)), radius_cells)
    lat_index = lax.axis_index("lat")
    lat_bands = lax.axis_size("lat")
    row_ids = jnp.arange(widened.shape[0])
    north_ok = jnp.logical_or(row_ids >= radius_cells, lat_index > 0)
    south_ok = jnp.logical_or(row_ids < widened.shape[0] - radius_cells, lat_index < lat_bands - 1)
    keep_rows = jnp.logical_and(north_ok, south_ok)
    return jnp.where(keep_rows[:, None, None], widened, jnp.zeros_like(widened))


def depthwise(padded, kernel, row_count, col_count):
    summed = jnp.zeros((row_count, col_count, padded.shape[2]), jnp.float32)
    for row_off in range(kernel.shape[0]):
        for col_off in range(kernel.shape[1]):
            window = padded[row_off : row_off + row_count, col_off : col_off + col_count].astype(
                jnp.float32
            )
            summed = summed + kernel[row_off, col_off].astype(jnp.float32) * window
    return summed


def back_conv(wide_grad, kernel, row_count, col_count):
    kernel_span = kernel.shape[0] - 1
    summed = jnp.zeros((row_count, col_count, wide_grad.shape[2]), jnp.float32)
    for row_off in range(kernel.shape[0]):
        for col_off in range(kernel.shape[1]):
            low_row = kernel_span - row_off
            low_col = kernel_span - col_off
            window = wide_grad[low_row : low_row + row_count, low_col : low_col + col_count].astype(
                jnp.float32
            )
            summed = summed + kernel[row_off, col_off].astype(jnp.float32) * window
    return summed


def kernel_terms(wide_field, grad_field, kernel_size):
    row_count = grad_field.shape[0]
    col_count = grad_field.shape[1]
    terms_list = []
    for row_off in range(kernel_size):
        for col_off in range(kernel_size):
            window = wide_field[
                row_off : row_off + row_count, col_off : col_off + col_count
            ].astype(jnp.float32)
            terms_list.append(jnp.sum(grad_field * window, axis=(0, 1)))
    return jnp.stack(terms_list).reshape(kernel_size, kernel_size, grad_field.shape[2])


def physics_forward(col_rows, column_in, column_out):
    column_pre = jnp.dot(col_rows, column_in, preferred_element_type=jnp.float32)
    inner = gelu_fn(column_pre).astype(jnp.bfloat16)
    state_full = col_rows.astype(jnp.float32) + jnp.dot(
        inner, column_out, preferred_element_type=jnp.float32
    )
    return (column_pre, inner, state_full)


def physics_backward(col_rows, column_pre, inner, target, column_in, column_out):
    inner_back = jnp.dot(target, column_out.T, preferred_element_type=jnp.float32)
    column_pre_grad = gelu_back(column_pre, inner_back).astype(jnp.bfloat16)
    column_grad = (
        target.astype(jnp.float32)
        + jnp.dot(column_pre_grad, column_in.T, preferred_element_type=jnp.float32)
    ).astype(jnp.bfloat16)
    grad_cin = jnp.dot(column_pre_grad.T, col_rows, preferred_element_type=jnp.float32)
    grad_cout = jnp.dot(inner.T, target, preferred_element_type=jnp.float32)
    return (column_grad, grad_cin, grad_cout)


def local(
    latent,
    ocean_mask,
    depth_kernel,
    expand_weight,
    reduce_weight,
    decode_weight,
    column_in,
    column_out,
    state_cot,
):
    tile_rows, tile_cols, channels = latent.shape
    cell_count = tile_rows * tile_cols
    col_width = state_cot.shape[2]
    device_count = lax.axis_size("lat") * lax.axis_size("lon")
    grad_scale = 1.0 / math.sqrt(cell_count * device_count)
    ocean = ocean_mask.astype(latent.dtype)
    masked = latent * ocean[:, :, None]
    wide_field = rim_field(masked)
    convolved = depthwise(wide_field, depth_kernel, tile_rows, tile_cols).reshape(
        cell_count, channels
    )
    row_mean = jnp.mean(convolved, axis=1, keepdims=True)
    centred = convolved - row_mean
    inverse_scale = lax.rsqrt(jnp.mean(centred * centred, axis=1, keepdims=True) + EPSILON)
    unit_rows = centred * inverse_scale
    normed = unit_rows.astype(jnp.bfloat16)
    expand_pre = jnp.dot(normed, expand_weight, preferred_element_type=jnp.float32)
    hidden = gelu_fn(expand_pre).astype(jnp.bfloat16)
    masked_flat = masked.reshape(cell_count, channels)
    feature = (
        masked_flat.astype(jnp.float32)
        + jnp.dot(hidden, reduce_weight, preferred_element_type=jnp.float32)
    ).astype(jnp.bfloat16)
    column = jnp.dot(feature, decode_weight, preferred_element_type=jnp.float32).astype(
        jnp.bfloat16
    )
    ocean_col = ocean_mask.reshape(cell_count, 1)
    cot_flat = state_cot.reshape(cell_count, col_width)
    column_pre, inner, state_full = physics_forward(column, column_in, column_out)
    state_home = jnp.where(ocean_col > 0, state_full, 0.0).astype(jnp.bfloat16)
    target = jnp.where(ocean_col > 0, cot_flat, jnp.zeros_like(cot_flat))
    column_grad, grad_cin, grad_cout = physics_backward(
        column, column_pre, inner, target, column_in, column_out
    )
    feature_back = jnp.dot(column_grad, decode_weight.T, preferred_element_type=jnp.float32)
    feature_grad = feature_back.astype(jnp.bfloat16)
    hidden_back = jnp.dot(feature_grad, reduce_weight.T, preferred_element_type=jnp.float32)
    expand_grad = gelu_back(expand_pre, hidden_back).astype(jnp.bfloat16)
    normed_back = jnp.dot(expand_grad, expand_weight.T, preferred_element_type=jnp.float32)
    conv_grad = (
        inverse_scale
        * (
            normed_back
            - jnp.mean(normed_back, axis=1, keepdims=True)
            - unit_rows * jnp.mean(normed_back * unit_rows, axis=1, keepdims=True)
        )
    ).astype(jnp.bfloat16)
    grad_decode = jnp.dot(feature.T, column_grad, preferred_element_type=jnp.float32)
    column_sums = shares_sum(
        (grad_cout, grad_cin, grad_decode), device_count, grad_scale
    )
    column_sums, conv_grad = lax.optimization_barrier((column_sums, conv_grad))
    conv_tile = conv_grad.reshape(tile_rows, tile_cols, channels)
    wide_grad = rim_field(conv_tile)
    grad_kernel = kernel_terms(wide_field, conv_tile.astype(jnp.float32), depth_kernel.shape[0])
    grad_expand = jnp.dot(expand_grad.T, normed, preferred_element_type=jnp.float32)
    grad_reduce = jnp.dot(hidden.T, feature_grad, preferred_element_type=jnp.float32)
    kernel_size = depth_kernel.shape[0]
    kernel_rows = jnp.moveaxis(
        grad_kernel.reshape(kernel_size, kernel_size, device_count, channels // device_count), 2, 0
    ).reshape(device_count, 1, -1)
    kernel_rows = jnp.pad(kernel_rows, ((0, 0), (0, 0), (0, channels - kernel_rows.shape[2])))
    mlp_rows, wide_grad = lax.optimization_barrier(
        ((grad_reduce, grad_expand, kernel_rows), wide_grad)
    )
    mlp_sums = shares_sum(mlp_rows, device_count, grad_scale)
    back_terms = back_conv(wide_grad, depth_kernel, tile_rows, tile_cols)
    grad_latent = (
        ocean_mask.astype(jnp.float32)[:, :, None]
        * (feature_back.reshape(tile_rows, tile_cols, channels) + back_terms)
    ).astype(jnp.bfloat16)
    kernel_share = channels // device_count
    state_out = state_home.reshape(tile_rows, tile_cols, col_width)
    return (
        state_out,
        grad_latent,
        mlp_sums[2][0, : kernel_size * kernel_size * kernel_share].reshape(
            kernel_size, kernel_size, kernel_share
        ),
        mlp_sums[1].T,
        mlp_sums[0],
        column_sums[2],
        column_sums[1].T,
        column_sums[0],
    )


def shares_sum(grads, device_count, grad_scale):
    rows = [grad.reshape(device_count, -1, grad.shape[-1]) for grad in grads]
    sizes = [row.shape[1] for row in rows]
    packed = jnp.concatenate(rows, axis=1)
    received = lax.all_to_all(packed, ("lat", "lon"), 0, 0, tiled=True)
    total = jnp.sum(received, axis=0) * grad_scale
    outs = []
    offset = 0
    for size in sizes:
        outs.append(total[offset : offset + size])
        offset += size
    return tuple(outs)


def solution(mesh):
    in_specs = (
        P("lat", "lon", None),
        P("lat", "lon"),
        P(),
        P(),
        P(),
        P(),
        P(),
        P(),
        P("lat", "lon", None),
    )
    out_specs = (
        P("lat", "lon", None),
        P("lat", "lon", None),
        P(None, None, ("lat", "lon")),
        P(None, ("lat", "lon")),
        P(("lat", "lon"), None),
        P(("lat", "lon"), None),
        P(None, ("lat", "lon")),
        P(("lat", "lon"), None),
    )
    return jax.shard_map(local, mesh=mesh, in_specs=in_specs, out_specs=out_specs, check_vma=False)
```

```python
import math

import jax
import jax.numpy as jnp
from jax import lax
from jax.sharding import Mesh
from jax.sharding import PartitionSpec as P

KERNEL = 7
LAT = ("y", "core")


EPSILON = 1e-06


def extended(cells, sides, width):
    for axis, dim in sides:
        count = lax.axis_size(axis)
        head = lax.slice_in_dim(cells, 0, width, axis=dim)
        tail = lax.slice_in_dim(cells, cells.shape[dim] - width, cells.shape[dim], axis=dim)
        cells = jnp.concatenate(
            [
                lax.ppermute(tail, axis, [(i, (i + 1) % count) for i in range(count)]),
                cells,
                lax.ppermute(head, axis, [((i + 1) % count, i) for i in range(count)]),
            ],
            axis=dim,
        )
    return cells


def gelu_fn(values_in):
    return jax.nn.gelu(values_in, approximate=True)


def gelu_back(pre_act, upstream):
    return jax.vjp(gelu_fn, pre_act)[1](upstream)[0]


def rim_field(tile_field):
    radius_cells = KERNEL // 2
    widened = extended(tile_field, ((LAT, 0), ("lon", 1)), radius_cells)
    lat_index = lax.axis_index(LAT)
    lat_bands = lax.axis_size(LAT)
    row_ids = jnp.arange(widened.shape[0])
    north_ok = jnp.logical_or(row_ids >= radius_cells, lat_index > 0)
    south_ok = jnp.logical_or(row_ids < widened.shape[0] - radius_cells, lat_index < lat_bands - 1)
    keep_rows = jnp.logical_and(north_ok, south_ok)
    return jnp.where(keep_rows[:, None, None], widened, jnp.zeros_like(widened))


def depthwise(padded, kernel, row_count, col_count):
    summed = jnp.zeros((row_count, col_count, padded.shape[2]), jnp.float32)
    for row_off in range(kernel.shape[0]):
        for col_off in range(kernel.shape[1]):
            window = padded[row_off : row_off + row_count, col_off : col_off + col_count].astype(
                jnp.float32
            )
            summed = summed + kernel[row_off, col_off].astype(jnp.float32) * window
    return summed


def back_conv(wide_grad, kernel, row_count, col_count):
    kernel_span = kernel.shape[0] - 1
    summed = jnp.zeros((row_count, col_count, wide_grad.shape[2]), jnp.float32)
    for row_off in range(kernel.shape[0]):
        for col_off in range(kernel.shape[1]):
            low_row = kernel_span - row_off
            low_col = kernel_span - col_off
            window = wide_grad[low_row : low_row + row_count, low_col : low_col + col_count].astype(
                jnp.float32
            )
            summed = summed + kernel[row_off, col_off].astype(jnp.float32) * window
    return summed


def kernel_terms(wide_field, grad_field, kernel_size):
    row_count = grad_field.shape[0]
    col_count = grad_field.shape[1]
    terms_list = []
    for row_off in range(kernel_size):
        for col_off in range(kernel_size):
            window = wide_field[
                row_off : row_off + row_count, col_off : col_off + col_count
            ].astype(jnp.float32)
            terms_list.append(jnp.sum(grad_field * window, axis=(0, 1)))
    return jnp.stack(terms_list).reshape(kernel_size, kernel_size, grad_field.shape[2])


def physics_forward(col_rows, column_in, column_out):
    column_pre = jnp.dot(col_rows, column_in, preferred_element_type=jnp.float32)
    inner = gelu_fn(column_pre).astype(jnp.bfloat16)
    state_full = col_rows.astype(jnp.float32) + jnp.dot(
        inner, column_out, preferred_element_type=jnp.float32
    )
    return (column_pre, inner, state_full)


def physics_backward(col_rows, column_pre, inner, target, column_in, column_out):
    inner_back = jnp.dot(target, column_out.T, preferred_element_type=jnp.float32)
    column_pre_grad = gelu_back(column_pre, inner_back).astype(jnp.bfloat16)
    column_grad = (
        target.astype(jnp.float32)
        + jnp.dot(column_pre_grad, column_in.T, preferred_element_type=jnp.float32)
    ).astype(jnp.bfloat16)
    grad_cin = jnp.dot(column_pre_grad.T, col_rows, preferred_element_type=jnp.float32)
    grad_cout = jnp.dot(inner.T, target, preferred_element_type=jnp.float32)
    return (column_grad, grad_cin, grad_cout)


def local(
    latent,
    ocean_mask,
    depth_kernel,
    expand_weight,
    reduce_weight,
    decode_weight,
    column_in,
    column_out,
    state_cot,
):
    tile_rows, tile_cols, channels = latent.shape
    cell_count = tile_rows * tile_cols
    col_width = state_cot.shape[2]
    device_count = lax.axis_size(LAT) * lax.axis_size("lon")
    grad_scale = 1.0 / math.sqrt(cell_count * device_count)
    ocean = ocean_mask.astype(latent.dtype)
    masked = latent * ocean[:, :, None]
    wide_field = rim_field(masked)
    convolved = depthwise(wide_field, depth_kernel, tile_rows, tile_cols).reshape(
        cell_count, channels
    )
    row_mean = jnp.mean(convolved, axis=1, keepdims=True)
    centred = convolved - row_mean
    inverse_scale = lax.rsqrt(jnp.mean(centred * centred, axis=1, keepdims=True) + EPSILON)
    unit_rows = centred * inverse_scale
    normed = unit_rows.astype(jnp.bfloat16)
    expand_pre = jnp.dot(normed, expand_weight, preferred_element_type=jnp.float32)
    hidden = gelu_fn(expand_pre).astype(jnp.bfloat16)
    masked_flat = masked.reshape(cell_count, channels)
    feature = (
        masked_flat.astype(jnp.float32)
        + jnp.dot(hidden, reduce_weight, preferred_element_type=jnp.float32)
    ).astype(jnp.bfloat16)
    column = jnp.dot(feature, decode_weight, preferred_element_type=jnp.float32).astype(
        jnp.bfloat16
    )
    ocean_col = ocean_mask.reshape(cell_count, 1)
    cot_flat = state_cot.reshape(cell_count, col_width)
    column_pre, inner, state_full = physics_forward(column, column_in, column_out)
    state_home = jnp.where(ocean_col > 0, state_full, 0.0).astype(jnp.bfloat16)
    target = jnp.where(ocean_col > 0, cot_flat, jnp.zeros_like(cot_flat))
    column_grad, grad_cin, grad_cout = physics_backward(
        column, column_pre, inner, target, column_in, column_out
    )
    feature_back = jnp.dot(column_grad, decode_weight.T, preferred_element_type=jnp.float32)
    feature_grad = feature_back.astype(jnp.bfloat16)
    hidden_back = jnp.dot(feature_grad, reduce_weight.T, preferred_element_type=jnp.float32)
    expand_grad = gelu_back(expand_pre, hidden_back).astype(jnp.bfloat16)
    normed_back = jnp.dot(expand_grad, expand_weight.T, preferred_element_type=jnp.float32)
    conv_grad = (
        inverse_scale
        * (
            normed_back
            - jnp.mean(normed_back, axis=1, keepdims=True)
            - unit_rows * jnp.mean(normed_back * unit_rows, axis=1, keepdims=True)
        )
    ).astype(jnp.bfloat16)
    grad_decode = jnp.dot(feature.T, column_grad, preferred_element_type=jnp.float32)
    column_sums = shares_sum(
        (grad_cout, grad_cin, grad_decode), device_count, grad_scale
    )
    column_sums, conv_grad = lax.optimization_barrier((column_sums, conv_grad))
    conv_tile = conv_grad.reshape(tile_rows, tile_cols, channels)
    wide_grad = rim_field(conv_tile)
    grad_kernel = kernel_terms(wide_field, conv_tile.astype(jnp.float32), depth_kernel.shape[0])
    grad_expand = jnp.dot(expand_grad.T, normed, preferred_element_type=jnp.float32)
    grad_reduce = jnp.dot(hidden.T, feature_grad, preferred_element_type=jnp.float32)
    kernel_size = depth_kernel.shape[0]
    kernel_rows = jnp.moveaxis(
        grad_kernel.reshape(kernel_size, kernel_size, device_count, channels // device_count), 2, 0
    ).reshape(device_count, 1, -1)
    kernel_rows = jnp.pad(kernel_rows, ((0, 0), (0, 0), (0, channels - kernel_rows.shape[2])))
    mlp_rows, wide_grad = lax.optimization_barrier(
        ((grad_reduce, grad_expand, kernel_rows), wide_grad)
    )
    mlp_sums = shares_sum(mlp_rows, device_count, grad_scale)
    back_terms = back_conv(wide_grad, depth_kernel, tile_rows, tile_cols)
    grad_latent = (
        ocean_mask.astype(jnp.float32)[:, :, None]
        * (feature_back.reshape(tile_rows, tile_cols, channels) + back_terms)
    ).astype(jnp.bfloat16)
    kernel_share = channels // device_count
    state_out = state_home.reshape(tile_rows, tile_cols, col_width)
    return (
        state_out,
        grad_latent,
        mlp_sums[2][0, : kernel_size * kernel_size * kernel_share].reshape(
            kernel_size, kernel_size, kernel_share
        ),
        mlp_sums[1].T,
        mlp_sums[0],
        column_sums[2],
        column_sums[1].T,
        column_sums[0],
    )


def shares_sum(grads, device_count, grad_scale):
    rows = [grad.reshape(device_count, -1, grad.shape[-1]) for grad in grads]
    sizes = [row.shape[1] for row in rows]
    packed = jnp.concatenate(rows, axis=1)
    cores = lax.axis_size("core")
    by_core = packed.reshape((-1, cores, device_count // (lax.axis_size("y") * cores)) + packed.shape[1:])
    core_index = lax.axis_index("core")
    kept = lax.dynamic_index_in_dim(by_core, core_index, axis=1, keepdims=False)
    given = lax.dynamic_index_in_dim(by_core, (core_index + 1) % cores, axis=1, keepdims=False)
    pairs = [(i, (i + 1) % cores) for i in range(cores)]
    chip_sum = kept + lax.ppermute(given, "core", pairs)
    chip_sum = chip_sum.reshape((-1,) + packed.shape[1:])
    received = lax.all_to_all(chip_sum, ("y", "lon"), 0, 0, tiled=True)
    total = jnp.sum(received, axis=0) * grad_scale
    outs = []
    offset = 0
    for size in sizes:
        outs.append(total[offset : offset + size])
        offset += size
    return tuple(outs)


def solution(mesh):
    lat_size, lon_size = mesh.devices.shape
    cores = 2
    chip_mesh = Mesh(
        mesh.devices.reshape(lat_size // cores, cores, lon_size), ("y", "core", "lon")
    )
    cells = P(LAT, "lon", None)
    every = (LAT[0], LAT[1], "lon")
    in_specs = (
        cells,
        P(LAT, "lon"),
        P(),
        P(),
        P(),
        P(),
        P(),
        P(),
        cells,
    )
    out_specs = (
        cells,
        cells,
        P(None, None, every),
        P(None, every),
        P(every, None),
        P(every, None),
        P(None, every),
        P(every, None),
    )
    return jax.shard_map(
        local, mesh=chip_mesh, in_specs=in_specs, out_specs=out_specs, check_vma=False
    )
```

```python
import math

import jax
import jax.numpy as jnp
from jax import lax
from jax.sharding import Mesh
from jax.sharding import PartitionSpec as P

KERNEL = 7
LAT = ("y", "core")


EPSILON = 1e-06


def extended(cells, sides, width):
    for axis, dim in sides:
        count = lax.axis_size(axis)
        head = lax.slice_in_dim(cells, 0, width, axis=dim)
        tail = lax.slice_in_dim(cells, cells.shape[dim] - width, cells.shape[dim], axis=dim)
        cells = jnp.concatenate(
            [
                lax.ppermute(tail, axis, [(i, (i + 1) % count) for i in range(count)]),
                cells,
                lax.ppermute(head, axis, [((i + 1) % count, i) for i in range(count)]),
            ],
            axis=dim,
        )
    return cells


def gelu_fn(values_in):
    return jax.nn.gelu(values_in, approximate=True)


def gelu_back(pre_act, upstream):
    return jax.vjp(gelu_fn, pre_act)[1](upstream)[0]


def rim_field(tile_field):
    radius_cells = KERNEL // 2
    widened = extended(tile_field, ((LAT, 0), ("lon", 1)), radius_cells)
    lat_index = lax.axis_index(LAT)
    lat_bands = lax.axis_size(LAT)
    row_ids = jnp.arange(widened.shape[0])
    north_ok = jnp.logical_or(row_ids >= radius_cells, lat_index > 0)
    south_ok = jnp.logical_or(row_ids < widened.shape[0] - radius_cells, lat_index < lat_bands - 1)
    keep_rows = jnp.logical_and(north_ok, south_ok)
    return jnp.where(keep_rows[:, None, None], widened, jnp.zeros_like(widened))


def depthwise(padded, kernel, row_count, col_count):
    summed = jnp.zeros((row_count, col_count, padded.shape[2]), jnp.float32)
    for row_off in range(kernel.shape[0]):
        for col_off in range(kernel.shape[1]):
            window = padded[row_off : row_off + row_count, col_off : col_off + col_count].astype(
                jnp.float32
            )
            summed = summed + kernel[row_off, col_off].astype(jnp.float32) * window
    return summed


def back_conv(wide_grad, kernel, row_count, col_count):
    kernel_span = kernel.shape[0] - 1
    summed = jnp.zeros((row_count, col_count, wide_grad.shape[2]), jnp.float32)
    for row_off in range(kernel.shape[0]):
        for col_off in range(kernel.shape[1]):
            low_row = kernel_span - row_off
            low_col = kernel_span - col_off
            window = wide_grad[low_row : low_row + row_count, low_col : low_col + col_count].astype(
                jnp.float32
            )
            summed = summed + kernel[row_off, col_off].astype(jnp.float32) * window
    return summed


def kernel_terms(wide_field, grad_field, kernel_size):
    row_count = grad_field.shape[0]
    col_count = grad_field.shape[1]
    terms_list = []
    for row_off in range(kernel_size):
        for col_off in range(kernel_size):
            window = wide_field[
                row_off : row_off + row_count, col_off : col_off + col_count
            ].astype(jnp.float32)
            terms_list.append(jnp.sum(grad_field * window, axis=(0, 1)))
    return jnp.stack(terms_list).reshape(kernel_size, kernel_size, grad_field.shape[2])


def physics_forward(col_rows, column_in, column_out):
    column_pre = jnp.dot(col_rows, column_in, preferred_element_type=jnp.float32)
    inner = gelu_fn(column_pre).astype(jnp.bfloat16)
    state_full = col_rows.astype(jnp.float32) + jnp.dot(
        inner, column_out, preferred_element_type=jnp.float32
    )
    return (column_pre, inner, state_full)


def physics_backward(col_rows, inner, target, column_in, column_out):
    inner_back = jnp.dot(target, column_out.T, preferred_element_type=jnp.float32)
    again_rows, again_in = lax.optimization_barrier((col_rows, column_in))
    column_pre = jnp.dot(again_rows, again_in, preferred_element_type=jnp.float32)
    column_pre_grad = gelu_back(column_pre, inner_back).astype(jnp.bfloat16)
    column_grad = (
        target.astype(jnp.float32)
        + jnp.dot(column_pre_grad, column_in.T, preferred_element_type=jnp.float32)
    ).astype(jnp.bfloat16)
    grad_cin = jnp.dot(column_pre_grad.T, col_rows, preferred_element_type=jnp.float32)
    grad_cout = jnp.dot(inner.T, target, preferred_element_type=jnp.float32)
    return (column_grad, grad_cin, grad_cout)


def local(
    latent,
    ocean_mask,
    depth_kernel,
    expand_weight,
    reduce_weight,
    decode_weight,
    column_in,
    column_out,
    state_cot,
):
    tile_rows, tile_cols, channels = latent.shape
    cell_count = tile_rows * tile_cols
    col_width = state_cot.shape[2]
    device_count = lax.axis_size(LAT) * lax.axis_size("lon")
    grad_scale = 1.0 / math.sqrt(cell_count * device_count)
    ocean = ocean_mask.astype(latent.dtype)
    masked = latent * ocean[:, :, None]
    wide_field = rim_field(masked)
    convolved = depthwise(wide_field, depth_kernel, tile_rows, tile_cols).reshape(
        cell_count, channels
    )
    row_mean = jnp.mean(convolved, axis=1, keepdims=True)
    centred = convolved - row_mean
    inverse_scale = lax.rsqrt(jnp.mean(centred * centred, axis=1, keepdims=True) + EPSILON)
    unit_rows = centred * inverse_scale
    normed = unit_rows.astype(jnp.bfloat16)
    expand_pre = jnp.dot(normed, expand_weight, preferred_element_type=jnp.float32)
    hidden = gelu_fn(expand_pre).astype(jnp.bfloat16)
    masked_flat = masked.reshape(cell_count, channels)
    feature = (
        masked_flat.astype(jnp.float32)
        + jnp.dot(hidden, reduce_weight, preferred_element_type=jnp.float32)
    ).astype(jnp.bfloat16)
    column = jnp.dot(feature, decode_weight, preferred_element_type=jnp.float32).astype(
        jnp.bfloat16
    )
    ocean_col = ocean_mask.reshape(cell_count, 1)
    cot_flat = state_cot.reshape(cell_count, col_width)
    _, inner, state_full = physics_forward(column, column_in, column_out)
    state_home = jnp.where(ocean_col > 0, state_full, 0.0).astype(jnp.bfloat16)
    target = jnp.where(ocean_col > 0, cot_flat, jnp.zeros_like(cot_flat))
    column_grad, grad_cin, grad_cout = physics_backward(
        column, inner, target, column_in, column_out
    )
    feature_back = jnp.dot(column_grad, decode_weight.T, preferred_element_type=jnp.float32)
    feature_grad = feature_back.astype(jnp.bfloat16)
    hidden_back = jnp.dot(feature_grad, reduce_weight.T, preferred_element_type=jnp.float32)
    expand_grad = gelu_back(expand_pre, hidden_back).astype(jnp.bfloat16)
    normed_back = jnp.dot(expand_grad, expand_weight.T, preferred_element_type=jnp.float32)
    conv_grad = (
        inverse_scale
        * (
            normed_back
            - jnp.mean(normed_back, axis=1, keepdims=True)
            - unit_rows * jnp.mean(normed_back * unit_rows, axis=1, keepdims=True)
        )
    ).astype(jnp.bfloat16)
    grad_decode = jnp.dot(feature.T, column_grad, preferred_element_type=jnp.float32)
    column_sums = shares_sum(
        (grad_cout, grad_cin, grad_decode), device_count, grad_scale
    )
    column_sums, conv_grad = lax.optimization_barrier((column_sums, conv_grad))
    conv_tile = conv_grad.reshape(tile_rows, tile_cols, channels)
    wide_grad = rim_field(conv_tile)
    grad_kernel = kernel_terms(wide_field, conv_tile.astype(jnp.float32), depth_kernel.shape[0])
    grad_expand = jnp.dot(expand_grad.T, normed, preferred_element_type=jnp.float32)
    grad_reduce = jnp.dot(hidden.T, feature_grad, preferred_element_type=jnp.float32)
    kernel_size = depth_kernel.shape[0]
    kernel_rows = jnp.moveaxis(
        grad_kernel.reshape(kernel_size, kernel_size, device_count, channels // device_count), 2, 0
    ).reshape(device_count, 1, -1)
    kernel_rows = jnp.pad(kernel_rows, ((0, 0), (0, 0), (0, channels - kernel_rows.shape[2])))
    mlp_rows, wide_grad = lax.optimization_barrier(
        ((grad_reduce, grad_expand, kernel_rows), wide_grad)
    )
    mlp_sums = shares_sum(mlp_rows, device_count, grad_scale)
    back_terms = back_conv(wide_grad, depth_kernel, tile_rows, tile_cols)
    grad_latent = (
        ocean_mask.astype(jnp.float32)[:, :, None]
        * (feature_back.reshape(tile_rows, tile_cols, channels) + back_terms)
    ).astype(jnp.bfloat16)
    kernel_share = channels // device_count
    state_out = state_home.reshape(tile_rows, tile_cols, col_width)
    return (
        state_out,
        grad_latent,
        mlp_sums[2][0, : kernel_size * kernel_size * kernel_share].reshape(
            kernel_size, kernel_size, kernel_share
        ),
        mlp_sums[1].T,
        mlp_sums[0],
        column_sums[2],
        column_sums[1].T,
        column_sums[0],
    )


def shares_sum(grads, device_count, grad_scale):
    rows = [grad.reshape(device_count, -1, grad.shape[-1]) for grad in grads]
    sizes = [row.shape[1] for row in rows]
    packed = jnp.concatenate(rows, axis=1)
    cores = lax.axis_size("core")
    by_core = packed.reshape((-1, cores, device_count // (lax.axis_size("y") * cores)) + packed.shape[1:])
    core_index = lax.axis_index("core")
    kept = lax.dynamic_index_in_dim(by_core, core_index, axis=1, keepdims=False)
    given = lax.dynamic_index_in_dim(by_core, (core_index + 1) % cores, axis=1, keepdims=False)
    pairs = [(i, (i + 1) % cores) for i in range(cores)]
    chip_sum = kept + lax.ppermute(given, "core", pairs)
    chip_sum = chip_sum.reshape((-1,) + packed.shape[1:])
    received = lax.all_to_all(chip_sum, ("y", "lon"), 0, 0, tiled=True)
    total = jnp.sum(received, axis=0) * grad_scale
    outs = []
    offset = 0
    for size in sizes:
        outs.append(total[offset : offset + size])
        offset += size
    return tuple(outs)


def solution(mesh):
    lat_size, lon_size = mesh.devices.shape
    cores = 2
    chip_mesh = Mesh(
        mesh.devices.reshape(lat_size // cores, cores, lon_size), ("y", "core", "lon")
    )
    cells = P(LAT, "lon", None)
    every = (LAT[0], LAT[1], "lon")
    in_specs = (
        cells,
        P(LAT, "lon"),
        P(),
        P(),
        P(),
        P(),
        P(),
        P(),
        cells,
    )
    out_specs = (
        cells,
        cells,
        P(None, None, every),
        P(None, every),
        P(every, None),
        P(every, None),
        P(None, every),
        P(every, None),
    )
    return jax.shard_map(
        local, mesh=chip_mesh, in_specs=in_specs, out_specs=out_specs, check_vma=False
    )
```

```python
import math

import jax
import jax.numpy as jnp
from jax import lax
from jax.sharding import Mesh
from jax.sharding import PartitionSpec as P

KERNEL = 7
LAT = ("y", "core")


EPSILON = 1e-06


def extended(cells, sides, width):
    for axis, dim in sides:
        count = lax.axis_size(axis)
        head = lax.slice_in_dim(cells, 0, width, axis=dim)
        tail = lax.slice_in_dim(cells, cells.shape[dim] - width, cells.shape[dim], axis=dim)
        cells = jnp.concatenate(
            [
                lax.ppermute(tail, axis, [(i, (i + 1) % count) for i in range(count)]),
                cells,
                lax.ppermute(head, axis, [((i + 1) % count, i) for i in range(count)]),
            ],
            axis=dim,
        )
    return cells


def gelu_fn(values_in):
    return jax.nn.gelu(values_in, approximate=True)


def gelu_back(pre_act, upstream):
    return jax.vjp(gelu_fn, pre_act)[1](upstream)[0]


def rim_field(tile_field):
    radius_cells = KERNEL // 2
    widened = extended(tile_field, ((LAT, 0), ("lon", 1)), radius_cells)
    lat_index = lax.axis_index(LAT)
    lat_bands = lax.axis_size(LAT)
    row_ids = jnp.arange(widened.shape[0])
    north_ok = jnp.logical_or(row_ids >= radius_cells, lat_index > 0)
    south_ok = jnp.logical_or(row_ids < widened.shape[0] - radius_cells, lat_index < lat_bands - 1)
    keep_rows = jnp.logical_and(north_ok, south_ok)
    return jnp.where(keep_rows[:, None, None], widened, jnp.zeros_like(widened))


def depthwise(padded, kernel, row_count, col_count):
    summed = jnp.zeros((row_count, col_count, padded.shape[2]), jnp.float32)
    for row_off in range(kernel.shape[0]):
        for col_off in range(kernel.shape[1]):
            window = padded[row_off : row_off + row_count, col_off : col_off + col_count].astype(
                jnp.float32
            )
            summed = summed + kernel[row_off, col_off].astype(jnp.float32) * window
    return summed


def back_conv(wide_grad, kernel, row_count, col_count):
    kernel_span = kernel.shape[0] - 1
    summed = jnp.zeros((row_count, col_count, wide_grad.shape[2]), jnp.float32)
    for row_off in range(kernel.shape[0]):
        for col_off in range(kernel.shape[1]):
            low_row = kernel_span - row_off
            low_col = kernel_span - col_off
            window = wide_grad[low_row : low_row + row_count, low_col : low_col + col_count].astype(
                jnp.float32
            )
            summed = summed + kernel[row_off, col_off].astype(jnp.float32) * window
    return summed


def kernel_terms(wide_field, grad_field, kernel_size):
    row_count = grad_field.shape[0]
    col_count = grad_field.shape[1]
    terms_list = []
    for row_off in range(kernel_size):
        for col_off in range(kernel_size):
            window = wide_field[
                row_off : row_off + row_count, col_off : col_off + col_count
            ].astype(jnp.float32)
            terms_list.append(jnp.sum(grad_field * window, axis=(0, 1)))
    return jnp.stack(terms_list).reshape(kernel_size, kernel_size, grad_field.shape[2])


def physics_forward(col_rows, column_in, column_out):
    column_pre = jnp.dot(col_rows, column_in, preferred_element_type=jnp.float32)
    inner = lax.optimization_barrier(gelu_fn(column_pre).astype(jnp.bfloat16))
    state_full = col_rows.astype(jnp.float32) + jnp.dot(
        inner, column_out, preferred_element_type=jnp.float32
    )
    return (column_pre, inner, state_full)


def physics_backward(col_rows, inner, target, column_in, column_out):
    inner_back = jnp.dot(target, column_out.T, preferred_element_type=jnp.float32)
    again_rows, again_in = lax.optimization_barrier((col_rows, column_in))
    column_pre = jnp.dot(again_rows, again_in, preferred_element_type=jnp.float32)
    column_pre_grad = gelu_back(column_pre, inner_back).astype(jnp.bfloat16)
    column_grad = (
        target.astype(jnp.float32)
        + jnp.dot(column_pre_grad, column_in.T, preferred_element_type=jnp.float32)
    ).astype(jnp.bfloat16)
    grad_cin = jnp.dot(column_pre_grad.T, col_rows, preferred_element_type=jnp.float32)
    grad_cout = jnp.dot(inner.T, target, preferred_element_type=jnp.float32)
    return (column_grad, grad_cin, grad_cout)


def local(
    latent,
    ocean_mask,
    depth_kernel,
    expand_weight,
    reduce_weight,
    decode_weight,
    column_in,
    column_out,
    state_cot,
):
    tile_rows, tile_cols, channels = latent.shape
    cell_count = tile_rows * tile_cols
    col_width = state_cot.shape[2]
    device_count = lax.axis_size(LAT) * lax.axis_size("lon")
    grad_scale = 1.0 / math.sqrt(cell_count * device_count)
    ocean = ocean_mask.astype(latent.dtype)
    masked = latent * ocean[:, :, None]
    wide_field = rim_field(masked)
    convolved = depthwise(wide_field, depth_kernel, tile_rows, tile_cols).reshape(
        cell_count, channels
    )
    row_mean = jnp.mean(convolved, axis=1, keepdims=True)
    centred = convolved - row_mean
    inverse_scale = lax.rsqrt(jnp.mean(centred * centred, axis=1, keepdims=True) + EPSILON)
    unit_rows = centred * inverse_scale
    normed = unit_rows.astype(jnp.bfloat16)
    expand_pre = jnp.dot(normed, expand_weight, preferred_element_type=jnp.float32)
    hidden = gelu_fn(expand_pre).astype(jnp.bfloat16)
    masked_flat = masked.reshape(cell_count, channels)
    feature = (
        masked_flat.astype(jnp.float32)
        + jnp.dot(hidden, reduce_weight, preferred_element_type=jnp.float32)
    ).astype(jnp.bfloat16)
    column = jnp.dot(feature, decode_weight, preferred_element_type=jnp.float32).astype(
        jnp.bfloat16
    )
    ocean_col = ocean_mask.reshape(cell_count, 1)
    cot_flat = state_cot.reshape(cell_count, col_width)
    _, inner, state_full = physics_forward(column, column_in, column_out)
    state_home = jnp.where(ocean_col > 0, state_full, 0.0).astype(jnp.bfloat16)
    target = jnp.where(ocean_col > 0, cot_flat, jnp.zeros_like(cot_flat))
    column_grad, grad_cin, grad_cout = physics_backward(
        column, inner, target, column_in, column_out
    )
    feature_back = jnp.dot(column_grad, decode_weight.T, preferred_element_type=jnp.float32)
    feature_grad = feature_back.astype(jnp.bfloat16)
    hidden_back = jnp.dot(feature_grad, reduce_weight.T, preferred_element_type=jnp.float32)
    expand_grad = gelu_back(expand_pre, hidden_back).astype(jnp.bfloat16)
    normed_back = jnp.dot(expand_grad, expand_weight.T, preferred_element_type=jnp.float32)
    conv_grad = (
        inverse_scale
        * (
            normed_back
            - jnp.mean(normed_back, axis=1, keepdims=True)
            - unit_rows * jnp.mean(normed_back * unit_rows, axis=1, keepdims=True)
        )
    ).astype(jnp.bfloat16)
    grad_decode = jnp.dot(feature.T, column_grad, preferred_element_type=jnp.float32)
    column_sums = shares_sum(
        (grad_cout, grad_cin, grad_decode), device_count, grad_scale
    )
    column_sums, conv_grad = lax.optimization_barrier((column_sums, conv_grad))
    conv_tile = conv_grad.reshape(tile_rows, tile_cols, channels)
    wide_grad = rim_field(conv_tile)
    grad_kernel = kernel_terms(wide_field, conv_tile.astype(jnp.float32), depth_kernel.shape[0])
    grad_expand = jnp.dot(expand_grad.T, normed, preferred_element_type=jnp.float32)
    grad_reduce = jnp.dot(hidden.T, feature_grad, preferred_element_type=jnp.float32)
    kernel_size = depth_kernel.shape[0]
    kernel_rows = jnp.moveaxis(
        grad_kernel.reshape(kernel_size, kernel_size, device_count, channels // device_count), 2, 0
    ).reshape(device_count, 1, -1)
    kernel_rows = jnp.pad(kernel_rows, ((0, 0), (0, 0), (0, channels - kernel_rows.shape[2])))
    mlp_rows, wide_grad = lax.optimization_barrier(
        ((grad_reduce, grad_expand, kernel_rows), wide_grad)
    )
    mlp_sums = shares_sum(mlp_rows, device_count, grad_scale)
    back_terms = back_conv(wide_grad, depth_kernel, tile_rows, tile_cols)
    grad_latent = (
        ocean_mask.astype(jnp.float32)[:, :, None]
        * (feature_back.reshape(tile_rows, tile_cols, channels) + back_terms)
    ).astype(jnp.bfloat16)
    kernel_share = channels // device_count
    state_out = state_home.reshape(tile_rows, tile_cols, col_width)
    return (
        state_out,
        grad_latent,
        mlp_sums[2][0, : kernel_size * kernel_size * kernel_share].reshape(
            kernel_size, kernel_size, kernel_share
        ),
        mlp_sums[1].T,
        mlp_sums[0],
        column_sums[2],
        column_sums[1].T,
        column_sums[0],
    )


def shares_sum(grads, device_count, grad_scale):
    rows = [grad.reshape(device_count, -1, grad.shape[-1]) for grad in grads]
    sizes = [row.shape[1] for row in rows]
    packed = jnp.concatenate(rows, axis=1)
    cores = lax.axis_size("core")
    by_core = packed.reshape((-1, cores, device_count // (lax.axis_size("y") * cores)) + packed.shape[1:])
    core_index = lax.axis_index("core")
    kept = lax.dynamic_index_in_dim(by_core, core_index, axis=1, keepdims=False)
    given = lax.dynamic_index_in_dim(by_core, (core_index + 1) % cores, axis=1, keepdims=False)
    pairs = [(i, (i + 1) % cores) for i in range(cores)]
    chip_sum = kept + lax.ppermute(given, "core", pairs)
    chip_sum = chip_sum.reshape((-1,) + packed.shape[1:])
    received = lax.all_to_all(chip_sum, ("y", "lon"), 0, 0, tiled=True)
    total = jnp.sum(received, axis=0) * grad_scale
    outs = []
    offset = 0
    for size in sizes:
        outs.append(total[offset : offset + size])
        offset += size
    return tuple(outs)


def solution(mesh):
    lat_size, lon_size = mesh.devices.shape
    cores = 2
    chip_mesh = Mesh(
        mesh.devices.reshape(lat_size // cores, cores, lon_size), ("y", "core", "lon")
    )
    cells = P(LAT, "lon", None)
    every = (LAT[0], LAT[1], "lon")
    in_specs = (
        cells,
        P(LAT, "lon"),
        P(),
        P(),
        P(),
        P(),
        P(),
        P(),
        cells,
    )
    out_specs = (
        cells,
        cells,
        P(None, None, every),
        P(None, every),
        P(every, None),
        P(every, None),
        P(None, every),
        P(every, None),
    )
    return jax.shard_map(
        local, mesh=chip_mesh, in_specs=in_specs, out_specs=out_specs, check_vma=False
    )
```

```python
import math

import jax
import jax.numpy as jnp
from jax import lax
from jax.sharding import Mesh
from jax.sharding import PartitionSpec as P

KERNEL = 7
LAT = ("y", "core")


EPSILON = 1e-06


def extended(cells, sides, width):
    for axis, dim in sides:
        count = lax.axis_size(axis)
        head = lax.slice_in_dim(cells, 0, width, axis=dim)
        tail = lax.slice_in_dim(cells, cells.shape[dim] - width, cells.shape[dim], axis=dim)
        cells = jnp.concatenate(
            [
                lax.ppermute(tail, axis, [(i, (i + 1) % count) for i in range(count)]),
                cells,
                lax.ppermute(head, axis, [((i + 1) % count, i) for i in range(count)]),
            ],
            axis=dim,
        )
    return cells


def gelu_fn(values_in):
    return jax.nn.gelu(values_in, approximate=True)


def gelu_back(pre_act, upstream):
    return jax.vjp(gelu_fn, pre_act)[1](upstream)[0]


def rim_field(tile_field):
    radius_cells = KERNEL // 2
    widened = extended(tile_field, ((LAT, 0), ("lon", 1)), radius_cells)
    lat_index = lax.axis_index(LAT)
    lat_bands = lax.axis_size(LAT)
    row_ids = jnp.arange(widened.shape[0])
    north_ok = jnp.logical_or(row_ids >= radius_cells, lat_index > 0)
    south_ok = jnp.logical_or(row_ids < widened.shape[0] - radius_cells, lat_index < lat_bands - 1)
    keep_rows = jnp.logical_and(north_ok, south_ok)
    return jnp.where(keep_rows[:, None, None], widened, jnp.zeros_like(widened))


def depthwise(padded, kernel, row_count, col_count):
    summed = jnp.zeros((row_count, col_count, padded.shape[2]), jnp.float32)
    for row_off in range(kernel.shape[0]):
        for col_off in range(kernel.shape[1]):
            window = padded[row_off : row_off + row_count, col_off : col_off + col_count].astype(
                jnp.float32
            )
            summed = summed + kernel[row_off, col_off].astype(jnp.float32) * window
    return summed


def back_conv(wide_grad, kernel, row_count, col_count):
    kernel_span = kernel.shape[0] - 1
    summed = jnp.zeros((row_count, col_count, wide_grad.shape[2]), jnp.float32)
    for row_off in range(kernel.shape[0]):
        for col_off in range(kernel.shape[1]):
            low_row = kernel_span - row_off
            low_col = kernel_span - col_off
            window = wide_grad[low_row : low_row + row_count, low_col : low_col + col_count].astype(
                jnp.float32
            )
            summed = summed + kernel[row_off, col_off].astype(jnp.float32) * window
    return summed


def kernel_terms(wide_field, grad_field, kernel_size):
    row_count = grad_field.shape[0]
    col_count = grad_field.shape[1]
    terms_list = []
    for row_off in range(kernel_size):
        for col_off in range(kernel_size):
            window = wide_field[
                row_off : row_off + row_count, col_off : col_off + col_count
            ].astype(jnp.float32)
            terms_list.append(jnp.sum(grad_field * window, axis=(0, 1)))
    return jnp.stack(terms_list).reshape(kernel_size, kernel_size, grad_field.shape[2])


def physics_forward(col_rows, column_in, column_out):
    column_pre = jnp.dot(col_rows, column_in, preferred_element_type=jnp.float32)
    inner = lax.optimization_barrier(gelu_fn(column_pre).astype(jnp.bfloat16))
    state_full = col_rows.astype(jnp.float32) + jnp.dot(
        inner, column_out, preferred_element_type=jnp.float32
    )
    return (column_pre, inner, state_full)


def physics_backward(col_rows, inner, target, column_in, column_out):
    inner_back = jnp.dot(target, column_out.T, preferred_element_type=jnp.float32)
    again_rows, again_in = lax.optimization_barrier((col_rows, column_in))
    column_pre = jnp.dot(again_rows, again_in, preferred_element_type=jnp.float32)
    column_pre_grad = gelu_back(column_pre, inner_back).astype(jnp.bfloat16)
    column_grad = (
        target.astype(jnp.float32)
        + jnp.dot(column_pre_grad, column_in.T, preferred_element_type=jnp.float32)
    ).astype(jnp.bfloat16)
    grad_cin = jnp.dot(column_pre_grad.T, col_rows, preferred_element_type=jnp.float32)
    grad_cout = jnp.dot(inner.T, target, preferred_element_type=jnp.float32)
    return (column_grad, grad_cin, grad_cout)


def local(
    latent,
    ocean_mask,
    depth_kernel,
    expand_weight,
    reduce_weight,
    decode_weight,
    column_in,
    column_out,
    state_cot,
):
    tile_rows, tile_cols, channels = latent.shape
    cell_count = tile_rows * tile_cols
    col_width = state_cot.shape[2]
    device_count = lax.axis_size(LAT) * lax.axis_size("lon")
    grad_scale = 1.0 / math.sqrt(cell_count * device_count)
    ocean = ocean_mask.astype(latent.dtype)
    masked = latent * ocean[:, :, None]
    wide_field = rim_field(masked)
    convolved = depthwise(wide_field, depth_kernel, tile_rows, tile_cols).reshape(
        cell_count, channels
    )
    row_mean = jnp.mean(convolved, axis=1, keepdims=True)
    centred = convolved - row_mean
    inverse_scale = lax.rsqrt(jnp.mean(centred * centred, axis=1, keepdims=True) + EPSILON)
    unit_rows = centred * inverse_scale
    normed = unit_rows.astype(jnp.bfloat16)
    expand_pre = jnp.dot(normed, expand_weight, preferred_element_type=jnp.float32)
    hidden = gelu_fn(expand_pre).astype(jnp.bfloat16)
    masked_flat = masked.reshape(cell_count, channels)
    feature = (
        masked_flat.astype(jnp.float32)
        + jnp.dot(hidden, reduce_weight, preferred_element_type=jnp.float32)
    ).astype(jnp.bfloat16)
    column = jnp.dot(feature, decode_weight, preferred_element_type=jnp.float32).astype(
        jnp.bfloat16
    )
    ocean_col = ocean_mask.reshape(cell_count, 1)
    cot_flat = state_cot.reshape(cell_count, col_width)
    _, inner, state_full = physics_forward(column, column_in, column_out)
    state_home = jnp.where(ocean_col > 0, state_full, 0.0).astype(jnp.bfloat16)
    target = jnp.where(ocean_col > 0, cot_flat, jnp.zeros_like(cot_flat))
    column_grad, grad_cin, grad_cout = physics_backward(
        column, inner, target, column_in, column_out
    )
    feature_back = jnp.dot(column_grad, decode_weight.T, preferred_element_type=jnp.float32)
    feature_grad = feature_back.astype(jnp.bfloat16)
    hidden_back = jnp.dot(feature_grad, reduce_weight.T, preferred_element_type=jnp.float32)
    expand_grad = gelu_back(expand_pre, hidden_back).astype(jnp.bfloat16)
    normed_back = jnp.dot(expand_grad, expand_weight.T, preferred_element_type=jnp.float32)
    conv_grad = (
        inverse_scale
        * (
            normed_back
            - jnp.mean(normed_back, axis=1, keepdims=True)
            - unit_rows * jnp.mean(normed_back * unit_rows, axis=1, keepdims=True)
        )
    ).astype(jnp.bfloat16)
    grad_decode = jnp.dot(feature.T, column_grad, preferred_element_type=jnp.float32)
    column_sums = shares_sum(
        (grad_cout, grad_cin, grad_decode), device_count, grad_scale
    )
    column_sums, conv_grad = lax.optimization_barrier((column_sums, conv_grad))
    conv_tile = conv_grad.reshape(tile_rows, tile_cols, channels)
    wide_grad = rim_field(conv_tile)
    grad_kernel = kernel_terms(wide_field, conv_tile.astype(jnp.float32), depth_kernel.shape[0])
    grad_expand = jnp.dot(expand_grad.T, normed, preferred_element_type=jnp.float32)
    grad_reduce = jnp.dot(hidden.T, feature_grad, preferred_element_type=jnp.float32)
    kernel_size = depth_kernel.shape[0]
    kernel_rows = jnp.moveaxis(
        grad_kernel.reshape(kernel_size, kernel_size, device_count, channels // device_count), 2, 0
    ).reshape(device_count, 1, -1)
    kernel_rows = jnp.pad(kernel_rows, ((0, 0), (0, 0), (0, channels - kernel_rows.shape[2])))
    mlp_rows, wide_grad = lax.optimization_barrier(
        ((grad_reduce, grad_expand, kernel_rows), wide_grad)
    )
    mlp_sums = shares_sum(mlp_rows, device_count, grad_scale)
    back_terms = back_conv(wide_grad, depth_kernel, tile_rows, tile_cols)
    grad_latent = (
        ocean_mask.astype(jnp.float32)[:, :, None]
        * (feature_back.reshape(tile_rows, tile_cols, channels) + back_terms)
    ).astype(jnp.bfloat16)
    kernel_share = channels // device_count
    state_out = state_home.reshape(tile_rows, tile_cols, col_width)
    return (
        state_out,
        grad_latent,
        mlp_sums[2][0, : kernel_size * kernel_size * kernel_share].reshape(
            kernel_size, kernel_size, kernel_share
        ),
        mlp_sums[1].T,
        mlp_sums[0],
        column_sums[2],
        column_sums[1].T,
        column_sums[0],
    )


def shares_sum(grads, device_count, grad_scale):
    rows = [grad.reshape(device_count, -1, grad.shape[-1]) for grad in grads]
    sizes = [row.shape[1] for row in rows]
    packed = jnp.concatenate(rows, axis=1)
    cores = lax.axis_size("core")
    by_core = packed.reshape((-1, cores, device_count // (lax.axis_size("y") * cores)) + packed.shape[1:])
    core_index = lax.axis_index("core")
    kept = lax.dynamic_index_in_dim(by_core, core_index, axis=1, keepdims=False)
    given = lax.dynamic_index_in_dim(by_core, (core_index + 1) % cores, axis=1, keepdims=False)
    pairs = [(i, (i + 1) % cores) for i in range(cores)]
    chip_sum = kept + lax.ppermute(given, "core", pairs)
    by_lon = jnp.swapaxes(chip_sum, 0, 1)
    lon_sum = jnp.sum(lax.all_to_all(by_lon, "lon", 0, 0, tiled=True), axis=0)
    total = jnp.sum(lax.all_to_all(lon_sum, "y", 0, 0, tiled=True), axis=0) * grad_scale
    outs = []
    offset = 0
    for size in sizes:
        outs.append(total[offset : offset + size])
        offset += size
    return tuple(outs)


def solution(mesh):
    lat_size, lon_size = mesh.devices.shape
    cores = 2
    chip_mesh = Mesh(
        mesh.devices.reshape(lat_size // cores, cores, lon_size), ("y", "core", "lon")
    )
    cells = P(LAT, "lon", None)
    every = (LAT[0], LAT[1], "lon")
    in_specs = (
        cells,
        P(LAT, "lon"),
        P(),
        P(),
        P(),
        P(),
        P(),
        P(),
        cells,
    )
    out_specs = (
        cells,
        cells,
        P(None, None, every),
        P(None, every),
        P(every, None),
        P(every, None),
        P(None, every),
        P(every, None),
    )
    return jax.shard_map(
        local, mesh=chip_mesh, in_specs=in_specs, out_specs=out_specs, check_vma=False
    )
```

```python
import math

import jax
import jax.numpy as jnp
from jax import lax
from jax.sharding import Mesh
from jax.sharding import PartitionSpec as P

KERNEL = 7
LAT = ("y", "core")


EPSILON = 1e-06


def extended(cells, sides, width):
    for axis, dim in sides:
        count = lax.axis_size(axis)
        head = lax.slice_in_dim(cells, 0, width, axis=dim)
        tail = lax.slice_in_dim(cells, cells.shape[dim] - width, cells.shape[dim], axis=dim)
        cells = jnp.concatenate(
            [
                lax.ppermute(tail, axis, [(i, (i + 1) % count) for i in range(count)]),
                cells,
                lax.ppermute(head, axis, [((i + 1) % count, i) for i in range(count)]),
            ],
            axis=dim,
        )
    return cells


def gelu_fn(values_in):
    return jax.nn.gelu(values_in, approximate=True)


def gelu_back(pre_act, upstream):
    return jax.vjp(gelu_fn, pre_act)[1](upstream)[0]


def rim_field(tile_field):
    radius_cells = KERNEL // 2
    widened = extended(tile_field, ((LAT, 0), ("lon", 1)), radius_cells)
    lat_index = lax.axis_index(LAT)
    lat_bands = lax.axis_size(LAT)
    row_ids = jnp.arange(widened.shape[0])
    north_ok = jnp.logical_or(row_ids >= radius_cells, lat_index > 0)
    south_ok = jnp.logical_or(row_ids < widened.shape[0] - radius_cells, lat_index < lat_bands - 1)
    keep_rows = jnp.logical_and(north_ok, south_ok)
    return jnp.where(keep_rows[:, None, None], widened, jnp.zeros_like(widened))


def depthwise(padded, kernel, row_count, col_count):
    summed = jnp.zeros((row_count, col_count, padded.shape[2]), jnp.float32)
    for row_off in range(kernel.shape[0]):
        for col_off in range(kernel.shape[1]):
            window = padded[row_off : row_off + row_count, col_off : col_off + col_count].astype(
                jnp.float32
            )
            summed = summed + kernel[row_off, col_off].astype(jnp.float32) * window
    return summed


def back_conv(wide_grad, kernel, row_count, col_count):
    kernel_span = kernel.shape[0] - 1
    summed = jnp.zeros((row_count, col_count, wide_grad.shape[2]), jnp.float32)
    for row_off in range(kernel.shape[0]):
        for col_off in range(kernel.shape[1]):
            low_row = kernel_span - row_off
            low_col = kernel_span - col_off
            window = wide_grad[low_row : low_row + row_count, low_col : low_col + col_count].astype(
                jnp.float32
            )
            summed = summed + kernel[row_off, col_off].astype(jnp.float32) * window
    return summed


def kernel_terms(wide_field, grad_field, kernel_size):
    row_count = grad_field.shape[0]
    col_count = grad_field.shape[1]
    terms_list = []
    for row_off in range(kernel_size):
        for col_off in range(kernel_size):
            window = wide_field[
                row_off : row_off + row_count, col_off : col_off + col_count
            ].astype(jnp.float32)
            terms_list.append(jnp.sum(grad_field * window, axis=(0, 1)))
    return jnp.stack(terms_list).reshape(kernel_size, kernel_size, grad_field.shape[2])


def physics_forward(col_rows, column_in, column_out):
    column_pre = jnp.dot(col_rows, column_in, preferred_element_type=jnp.float32)
    inner = lax.optimization_barrier(gelu_fn(column_pre).astype(jnp.bfloat16))
    state_full = col_rows.astype(jnp.float32) + jnp.dot(
        inner, column_out, preferred_element_type=jnp.float32
    )
    return (column_pre, inner, state_full)


def physics_backward(col_rows, inner, target, column_in, column_out):
    inner_back = jnp.dot(target, column_out.T, preferred_element_type=jnp.float32)
    again_rows, again_in = lax.optimization_barrier((col_rows, column_in))
    column_pre = jnp.dot(again_rows, again_in, preferred_element_type=jnp.float32)
    column_pre_grad = gelu_back(column_pre, inner_back).astype(jnp.bfloat16)
    column_grad = (
        target.astype(jnp.float32)
        + jnp.dot(column_pre_grad, column_in.T, preferred_element_type=jnp.float32)
    ).astype(jnp.bfloat16)
    grad_cin = jnp.dot(column_pre_grad.T, col_rows, preferred_element_type=jnp.float32)
    grad_cout = jnp.dot(inner.T, target, preferred_element_type=jnp.float32)
    return (column_grad, grad_cin, grad_cout)


def local(
    latent,
    ocean_mask,
    depth_kernel,
    expand_weight,
    reduce_weight,
    decode_weight,
    column_in,
    column_out,
    state_cot,
):
    tile_rows, tile_cols, channels = latent.shape
    cell_count = tile_rows * tile_cols
    col_width = state_cot.shape[2]
    device_count = lax.axis_size(LAT) * lax.axis_size("lon")
    grad_scale = 1.0 / math.sqrt(cell_count * device_count)
    ocean = ocean_mask.astype(latent.dtype)
    masked = latent * ocean[:, :, None]
    wide_field = rim_field(masked)
    convolved = depthwise(wide_field, depth_kernel, tile_rows, tile_cols).reshape(
        cell_count, channels
    )
    row_mean = jnp.mean(convolved, axis=1, keepdims=True)
    centred = convolved - row_mean
    inverse_scale = lax.rsqrt(jnp.mean(centred * centred, axis=1, keepdims=True) + EPSILON)
    unit_rows = centred * inverse_scale
    normed = unit_rows.astype(jnp.bfloat16)
    expand_pre = jnp.dot(normed, expand_weight, preferred_element_type=jnp.float32)
    hidden = gelu_fn(expand_pre).astype(jnp.bfloat16)
    masked_flat = masked.reshape(cell_count, channels)
    feature = (
        masked_flat.astype(jnp.float32)
        + jnp.dot(hidden, reduce_weight, preferred_element_type=jnp.float32)
    ).astype(jnp.bfloat16)
    column = jnp.dot(feature, decode_weight, preferred_element_type=jnp.float32).astype(
        jnp.bfloat16
    )
    ocean_col = ocean_mask.reshape(cell_count, 1)
    cot_flat = state_cot.reshape(cell_count, col_width)
    _, inner, state_full = physics_forward(column, column_in, column_out)
    state_home = jnp.where(ocean_col > 0, state_full, 0.0).astype(jnp.bfloat16)
    target = jnp.where(ocean_col > 0, cot_flat, jnp.zeros_like(cot_flat))
    column_grad, grad_cin, grad_cout = physics_backward(
        column, inner, target, column_in, column_out
    )
    feature_back = jnp.dot(column_grad, decode_weight.T, preferred_element_type=jnp.float32)
    feature_grad = feature_back.astype(jnp.bfloat16)
    hidden_back = jnp.dot(feature_grad, reduce_weight.T, preferred_element_type=jnp.float32)
    expand_grad = gelu_back(expand_pre, hidden_back).astype(jnp.bfloat16)
    normed_back = jnp.dot(expand_grad, expand_weight.T, preferred_element_type=jnp.float32)
    conv_grad = (
        inverse_scale
        * (
            normed_back
            - jnp.mean(normed_back, axis=1, keepdims=True)
            - unit_rows * jnp.mean(normed_back * unit_rows, axis=1, keepdims=True)
        )
    ).astype(jnp.bfloat16)
    grad_decode = jnp.dot(feature.T, column_grad, preferred_element_type=jnp.float32)
    column_sums = shares_sum(
        (grad_cout, grad_cin, grad_decode), device_count, grad_scale
    )
    column_sums, conv_grad = lax.optimization_barrier((column_sums, conv_grad))
    conv_tile = conv_grad.reshape(tile_rows, tile_cols, channels)
    wide_grad = rim_field(conv_tile)
    grad_kernel = kernel_terms(wide_field, conv_tile.astype(jnp.float32), depth_kernel.shape[0])
    grad_expand = jnp.dot(expand_grad.T, normed, preferred_element_type=jnp.float32)
    grad_reduce = jnp.dot(hidden.T, feature_grad, preferred_element_type=jnp.float32)
    kernel_size = depth_kernel.shape[0]
    kernel_rows = jnp.moveaxis(
        grad_kernel.reshape(kernel_size, kernel_size, device_count, channels // device_count), 2, 0
    ).reshape(device_count, 1, -1)
    kernel_rows = jnp.pad(kernel_rows, ((0, 0), (0, 0), (0, channels - kernel_rows.shape[2])))
    mlp_rows, wide_grad = lax.optimization_barrier(
        ((grad_reduce, grad_expand, kernel_rows), wide_grad)
    )
    mlp_sums = shares_sum(mlp_rows, device_count, grad_scale)
    back_terms = back_conv(wide_grad, depth_kernel, tile_rows, tile_cols)
    grad_latent = (
        ocean_mask.astype(jnp.float32)[:, :, None]
        * (feature_back.reshape(tile_rows, tile_cols, channels) + back_terms)
    ).astype(jnp.bfloat16)
    kernel_share = channels // device_count
    state_out = state_home.reshape(tile_rows, tile_cols, col_width)
    return (
        state_out,
        grad_latent,
        mlp_sums[2][0, : kernel_size * kernel_size * kernel_share].reshape(
            kernel_size, kernel_size, kernel_share
        ),
        mlp_sums[1].T,
        mlp_sums[0],
        column_sums[2],
        column_sums[1].T,
        column_sums[0],
    )


def shares_sum(grads, device_count, grad_scale):
    rows = [grad.reshape(device_count, -1, grad.shape[-1]) for grad in grads]
    sizes = [row.shape[1] for row in rows]
    packed = jnp.concatenate(rows, axis=1)
    cores = lax.axis_size("core")
    by_core = packed.reshape((-1, cores, device_count // (lax.axis_size("y") * cores)) + packed.shape[1:])
    core_index = lax.axis_index("core")
    first = core_index == 0
    kept = jnp.where(first, by_core[:, 0], by_core[:, 1])
    given = jnp.where(first, by_core[:, 1], by_core[:, 0])
    pairs = [(i, (i + 1) % cores) for i in range(cores)]
    chip_sum = kept + lax.ppermute(given, "core", pairs)
    chip_sum = chip_sum.reshape((-1,) + packed.shape[1:])
    received = lax.all_to_all(chip_sum, ("y", "lon"), 0, 0, tiled=True)
    total = jnp.sum(received, axis=0) * grad_scale
    outs = []
    offset = 0
    for size in sizes:
        outs.append(total[offset : offset + size])
        offset += size
    return tuple(outs)


def solution(mesh):
    lat_size, lon_size = mesh.devices.shape
    cores = 2
    chip_mesh = Mesh(
        mesh.devices.reshape(lat_size // cores, cores, lon_size), ("y", "core", "lon")
    )
    cells = P(LAT, "lon", None)
    every = (LAT[0], LAT[1], "lon")
    in_specs = (
        cells,
        P(LAT, "lon"),
        P(),
        P(),
        P(),
        P(),
        P(),
        P(),
        cells,
    )
    out_specs = (
        cells,
        cells,
        P(None, None, every),
        P(None, every),
        P(every, None),
        P(every, None),
        P(None, every),
        P(every, None),
    )
    return jax.shard_map(
        local, mesh=chip_mesh, in_specs=in_specs, out_specs=out_specs, check_vma=False
    )
```

```python
import math

import jax
import jax.numpy as jnp
from jax import lax
from jax.sharding import Mesh
from jax.sharding import PartitionSpec as P

KERNEL = 7
LAT = ("y", "core")


EPSILON = 1e-06


def extended(cells, sides, width):
    for axis, dim in sides:
        count = lax.axis_size(axis)
        head = lax.slice_in_dim(cells, 0, width, axis=dim)
        tail = lax.slice_in_dim(cells, cells.shape[dim] - width, cells.shape[dim], axis=dim)
        cells = jnp.concatenate(
            [
                lax.ppermute(tail, axis, [(i, (i + 1) % count) for i in range(count)]),
                cells,
                lax.ppermute(head, axis, [((i + 1) % count, i) for i in range(count)]),
            ],
            axis=dim,
        )
    return cells


def gelu_fn(values_in):
    return jax.nn.gelu(values_in, approximate=True)


def gelu_back(pre_act, upstream):
    return jax.vjp(gelu_fn, pre_act)[1](upstream)[0]


def rim_field(tile_field):
    radius_cells = KERNEL // 2
    widened = extended(tile_field, (("lon", 1), (LAT, 0)), radius_cells)
    lat_index = lax.axis_index(LAT)
    lat_bands = lax.axis_size(LAT)
    row_ids = jnp.arange(widened.shape[0])
    north_ok = jnp.logical_or(row_ids >= radius_cells, lat_index > 0)
    south_ok = jnp.logical_or(row_ids < widened.shape[0] - radius_cells, lat_index < lat_bands - 1)
    keep_rows = jnp.logical_and(north_ok, south_ok)
    return jnp.where(keep_rows[:, None, None], widened, jnp.zeros_like(widened))


def depthwise(padded, kernel, row_count, col_count):
    summed = jnp.zeros((row_count, col_count, padded.shape[2]), jnp.float32)
    for row_off in range(kernel.shape[0]):
        for col_off in range(kernel.shape[1]):
            window = padded[row_off : row_off + row_count, col_off : col_off + col_count].astype(
                jnp.float32
            )
            summed = summed + kernel[row_off, col_off].astype(jnp.float32) * window
    return summed


def back_conv(wide_grad, kernel, row_count, col_count):
    kernel_span = kernel.shape[0] - 1
    summed = jnp.zeros((row_count, col_count, wide_grad.shape[2]), jnp.float32)
    for row_off in range(kernel.shape[0]):
        for col_off in range(kernel.shape[1]):
            low_row = kernel_span - row_off
            low_col = kernel_span - col_off
            window = wide_grad[low_row : low_row + row_count, low_col : low_col + col_count].astype(
                jnp.float32
            )
            summed = summed + kernel[row_off, col_off].astype(jnp.float32) * window
    return summed


def kernel_terms(wide_field, grad_field, kernel_size):
    row_count = grad_field.shape[0]
    col_count = grad_field.shape[1]
    terms_list = []
    for row_off in range(kernel_size):
        for col_off in range(kernel_size):
            window = wide_field[
                row_off : row_off + row_count, col_off : col_off + col_count
            ].astype(jnp.float32)
            terms_list.append(jnp.sum(grad_field * window, axis=(0, 1)))
    return jnp.stack(terms_list).reshape(kernel_size, kernel_size, grad_field.shape[2])


def physics_forward(col_rows, column_in, column_out):
    column_pre = jnp.dot(col_rows, column_in, preferred_element_type=jnp.float32)
    inner = lax.optimization_barrier(gelu_fn(column_pre).astype(jnp.bfloat16))
    state_full = col_rows.astype(jnp.float32) + jnp.dot(
        inner, column_out, preferred_element_type=jnp.float32
    )
    return (column_pre, inner, state_full)


def physics_backward(col_rows, inner, target, column_in, column_out):
    inner_back = jnp.dot(target, column_out.T, preferred_element_type=jnp.float32)
    again_rows, again_in = lax.optimization_barrier((col_rows, column_in))
    column_pre = jnp.dot(again_rows, again_in, preferred_element_type=jnp.float32)
    column_pre_grad = gelu_back(column_pre, inner_back).astype(jnp.bfloat16)
    column_grad = (
        target.astype(jnp.float32)
        + jnp.dot(column_pre_grad, column_in.T, preferred_element_type=jnp.float32)
    ).astype(jnp.bfloat16)
    grad_cin = jnp.dot(column_pre_grad.T, col_rows, preferred_element_type=jnp.float32)
    grad_cout = jnp.dot(inner.T, target, preferred_element_type=jnp.float32)
    return (column_grad, grad_cin, grad_cout)


def local(
    latent,
    ocean_mask,
    depth_kernel,
    expand_weight,
    reduce_weight,
    decode_weight,
    column_in,
    column_out,
    state_cot,
):
    tile_rows, tile_cols, channels = latent.shape
    cell_count = tile_rows * tile_cols
    col_width = state_cot.shape[2]
    device_count = lax.axis_size(LAT) * lax.axis_size("lon")
    grad_scale = 1.0 / math.sqrt(cell_count * device_count)
    ocean = ocean_mask.astype(latent.dtype)
    masked = latent * ocean[:, :, None]
    wide_field = rim_field(masked)
    convolved = depthwise(wide_field, depth_kernel, tile_rows, tile_cols).reshape(
        cell_count, channels
    )
    row_mean = jnp.mean(convolved, axis=1, keepdims=True)
    centred = convolved - row_mean
    inverse_scale = lax.rsqrt(jnp.mean(centred * centred, axis=1, keepdims=True) + EPSILON)
    unit_rows = centred * inverse_scale
    normed = unit_rows.astype(jnp.bfloat16)
    expand_pre = jnp.dot(normed, expand_weight, preferred_element_type=jnp.float32)
    hidden = gelu_fn(expand_pre).astype(jnp.bfloat16)
    masked_flat = masked.reshape(cell_count, channels)
    feature = (
        masked_flat.astype(jnp.float32)
        + jnp.dot(hidden, reduce_weight, preferred_element_type=jnp.float32)
    ).astype(jnp.bfloat16)
    column = jnp.dot(feature, decode_weight, preferred_element_type=jnp.float32).astype(
        jnp.bfloat16
    )
    ocean_col = ocean_mask.reshape(cell_count, 1)
    cot_flat = state_cot.reshape(cell_count, col_width)
    _, inner, state_full = physics_forward(column, column_in, column_out)
    state_home = jnp.where(ocean_col > 0, state_full, 0.0).astype(jnp.bfloat16)
    target = jnp.where(ocean_col > 0, cot_flat, jnp.zeros_like(cot_flat))
    column_grad, grad_cin, grad_cout = physics_backward(
        column, inner, target, column_in, column_out
    )
    feature_back = jnp.dot(column_grad, decode_weight.T, preferred_element_type=jnp.float32)
    feature_grad = feature_back.astype(jnp.bfloat16)
    hidden_back = jnp.dot(feature_grad, reduce_weight.T, preferred_element_type=jnp.float32)
    expand_grad = gelu_back(expand_pre, hidden_back).astype(jnp.bfloat16)
    normed_back = jnp.dot(expand_grad, expand_weight.T, preferred_element_type=jnp.float32)
    conv_grad = (
        inverse_scale
        * (
            normed_back
            - jnp.mean(normed_back, axis=1, keepdims=True)
            - unit_rows * jnp.mean(normed_back * unit_rows, axis=1, keepdims=True)
        )
    ).astype(jnp.bfloat16)
    grad_decode = jnp.dot(feature.T, column_grad, preferred_element_type=jnp.float32)
    column_sums = shares_sum(
        (grad_cout, grad_cin, grad_decode), device_count, grad_scale
    )
    column_sums, conv_grad = lax.optimization_barrier((column_sums, conv_grad))
    conv_tile = conv_grad.reshape(tile_rows, tile_cols, channels)
    wide_grad = rim_field(conv_tile)
    grad_kernel = kernel_terms(wide_field, conv_tile.astype(jnp.float32), depth_kernel.shape[0])
    grad_expand = jnp.dot(expand_grad.T, normed, preferred_element_type=jnp.float32)
    grad_reduce = jnp.dot(hidden.T, feature_grad, preferred_element_type=jnp.float32)
    kernel_size = depth_kernel.shape[0]
    kernel_rows = jnp.moveaxis(
        grad_kernel.reshape(kernel_size, kernel_size, device_count, channels // device_count), 2, 0
    ).reshape(device_count, 1, -1)
    kernel_rows = jnp.pad(kernel_rows, ((0, 0), (0, 0), (0, channels - kernel_rows.shape[2])))
    mlp_rows, wide_grad = lax.optimization_barrier(
        ((grad_reduce, grad_expand, kernel_rows), wide_grad)
    )
    mlp_sums = shares_sum(mlp_rows, device_count, grad_scale)
    back_terms = back_conv(wide_grad, depth_kernel, tile_rows, tile_cols)
    grad_latent = (
        ocean_mask.astype(jnp.float32)[:, :, None]
        * (feature_back.reshape(tile_rows, tile_cols, channels) + back_terms)
    ).astype(jnp.bfloat16)
    kernel_share = channels // device_count
    state_out = state_home.reshape(tile_rows, tile_cols, col_width)
    return (
        state_out,
        grad_latent,
        mlp_sums[2][0, : kernel_size * kernel_size * kernel_share].reshape(
            kernel_size, kernel_size, kernel_share
        ),
        mlp_sums[1].T,
        mlp_sums[0],
        column_sums[2],
        column_sums[1].T,
        column_sums[0],
    )


def shares_sum(grads, device_count, grad_scale):
    rows = [grad.reshape(device_count, -1, grad.shape[-1]) for grad in grads]
    sizes = [row.shape[1] for row in rows]
    packed = jnp.concatenate(rows, axis=1)
    cores = lax.axis_size("core")
    by_core = packed.reshape((-1, cores, device_count // (lax.axis_size("y") * cores)) + packed.shape[1:])
    core_index = lax.axis_index("core")
    first = core_index == 0
    kept = jnp.where(first, by_core[:, 0], by_core[:, 1])
    given = jnp.where(first, by_core[:, 1], by_core[:, 0])
    pairs = [(i, (i + 1) % cores) for i in range(cores)]
    chip_sum = kept + lax.ppermute(given, "core", pairs)
    chip_sum = chip_sum.reshape((-1,) + packed.shape[1:])
    received = lax.all_to_all(chip_sum, ("y", "lon"), 0, 0, tiled=True)
    total = jnp.sum(received, axis=0) * grad_scale
    outs = []
    offset = 0
    for size in sizes:
        outs.append(total[offset : offset + size])
        offset += size
    return tuple(outs)


def solution(mesh):
    lat_size, lon_size = mesh.devices.shape
    cores = 2
    chip_mesh = Mesh(
        mesh.devices.reshape(lat_size // cores, cores, lon_size), ("y", "core", "lon")
    )
    cells = P(LAT, "lon", None)
    every = (LAT[0], LAT[1], "lon")
    in_specs = (
        cells,
        P(LAT, "lon"),
        P(),
        P(),
        P(),
        P(),
        P(),
        P(),
        cells,
    )
    out_specs = (
        cells,
        cells,
        P(None, None, every),
        P(None, every),
        P(every, None),
        P(every, None),
        P(None, every),
        P(every, None),
    )
    return jax.shard_map(
        local, mesh=chip_mesh, in_specs=in_specs, out_specs=out_specs, check_vma=False
    )
```

```python
import math

import jax
import jax.numpy as jnp
from jax import lax
from jax.sharding import Mesh
from jax.sharding import PartitionSpec as P

KERNEL = 7
LAT = ("y", "core")


EPSILON = 1e-06


def extended(cells, sides, width):
    for axis, dim in sides:
        count = lax.axis_size(axis)
        head = lax.slice_in_dim(cells, 0, width, axis=dim)
        tail = lax.slice_in_dim(cells, cells.shape[dim] - width, cells.shape[dim], axis=dim)
        cells = jnp.concatenate(
            [
                lax.ppermute(tail, axis, [(i, (i + 1) % count) for i in range(count)]),
                cells,
                lax.ppermute(head, axis, [((i + 1) % count, i) for i in range(count)]),
            ],
            axis=dim,
        )
    return cells


def gelu_fn(values_in):
    return jax.nn.gelu(values_in, approximate=True)


def gelu_back(pre_act, upstream):
    return jax.vjp(gelu_fn, pre_act)[1](upstream)[0]


def rim_field(tile_field):
    radius_cells = KERNEL // 2
    widened = extended(tile_field, ((LAT, 0), ("lon", 1)), radius_cells)
    lat_index = lax.axis_index(LAT)
    lat_bands = lax.axis_size(LAT)
    row_ids = jnp.arange(widened.shape[0])
    north_ok = jnp.logical_or(row_ids >= radius_cells, lat_index > 0)
    south_ok = jnp.logical_or(row_ids < widened.shape[0] - radius_cells, lat_index < lat_bands - 1)
    keep_rows = jnp.logical_and(north_ok, south_ok)
    return jnp.where(keep_rows[:, None, None], widened, jnp.zeros_like(widened))


def depthwise(padded, kernel, row_count, col_count):
    summed = jnp.zeros((row_count, col_count, padded.shape[2]), jnp.float32)
    for row_off in range(kernel.shape[0]):
        for col_off in range(kernel.shape[1]):
            window = padded[row_off : row_off + row_count, col_off : col_off + col_count].astype(
                jnp.float32
            )
            summed = summed + kernel[row_off, col_off].astype(jnp.float32) * window
    return summed


def back_conv(wide_grad, kernel, row_count, col_count):
    kernel_span = kernel.shape[0] - 1
    summed = jnp.zeros((row_count, col_count, wide_grad.shape[2]), jnp.float32)
    for row_off in range(kernel.shape[0]):
        for col_off in range(kernel.shape[1]):
            low_row = kernel_span - row_off
            low_col = kernel_span - col_off
            window = wide_grad[low_row : low_row + row_count, low_col : low_col + col_count].astype(
                jnp.float32
            )
            summed = summed + kernel[row_off, col_off].astype(jnp.float32) * window
    return summed


def kernel_terms(wide_field, grad_field, kernel_size):
    row_count = grad_field.shape[0]
    col_count = grad_field.shape[1]
    terms_list = []
    for row_off in range(kernel_size):
        for col_off in range(kernel_size):
            window = wide_field[
                row_off : row_off + row_count, col_off : col_off + col_count
            ].astype(jnp.float32)
            terms_list.append(jnp.sum(grad_field * window, axis=(0, 1)))
    return jnp.stack(terms_list).reshape(kernel_size, kernel_size, grad_field.shape[2])


def physics_forward(col_rows, column_in, column_out):
    column_pre = jnp.dot(col_rows, column_in, preferred_element_type=jnp.float32)
    inner = lax.optimization_barrier(gelu_fn(column_pre).astype(jnp.bfloat16))
    state_full = col_rows.astype(jnp.float32) + jnp.dot(
        inner, column_out, preferred_element_type=jnp.float32
    )
    return (column_pre, inner, state_full)


def physics_backward(col_rows, inner, target, column_in, column_out):
    inner_back = jnp.dot(target, column_out.T, preferred_element_type=jnp.float32)
    again_rows, again_in = lax.optimization_barrier((col_rows, column_in))
    column_pre = jnp.dot(again_rows, again_in, preferred_element_type=jnp.float32)
    column_pre_grad = gelu_back(column_pre, inner_back).astype(jnp.bfloat16)
    column_grad = (
        target.astype(jnp.float32)
        + jnp.dot(column_pre_grad, column_in.T, preferred_element_type=jnp.float32)
    ).astype(jnp.bfloat16)
    grad_cin = jnp.dot(column_pre_grad.T, col_rows, preferred_element_type=jnp.float32)
    grad_cout = jnp.dot(inner.T, target, preferred_element_type=jnp.float32)
    return (column_grad, grad_cin, grad_cout)


def local(
    latent,
    ocean_mask,
    depth_kernel,
    expand_weight,
    reduce_weight,
    decode_weight,
    column_in,
    column_out,
    state_cot,
):
    tile_rows, tile_cols, channels = latent.shape
    cell_count = tile_rows * tile_cols
    col_width = state_cot.shape[2]
    device_count = lax.axis_size(LAT) * lax.axis_size("lon")
    grad_scale = 1.0 / math.sqrt(cell_count * device_count)
    ocean = ocean_mask.astype(latent.dtype)
    masked = latent * ocean[:, :, None]
    wide_field = rim_field(masked)
    convolved = depthwise(wide_field, depth_kernel, tile_rows, tile_cols).reshape(
        cell_count, channels
    )
    row_mean = jnp.mean(convolved, axis=1, keepdims=True)
    centred = convolved - row_mean
    inverse_scale = lax.rsqrt(jnp.mean(centred * centred, axis=1, keepdims=True) + EPSILON)
    unit_rows = centred * inverse_scale
    normed = unit_rows.astype(jnp.bfloat16)
    expand_pre = jnp.dot(normed, expand_weight, preferred_element_type=jnp.float32)
    hidden = lax.optimization_barrier(gelu_fn(expand_pre).astype(jnp.bfloat16))
    masked_flat = masked.reshape(cell_count, channels)
    feature = (
        masked_flat.astype(jnp.float32)
        + jnp.dot(hidden, reduce_weight, preferred_element_type=jnp.float32)
    ).astype(jnp.bfloat16)
    column = jnp.dot(feature, decode_weight, preferred_element_type=jnp.float32).astype(
        jnp.bfloat16
    )
    ocean_col = ocean_mask.reshape(cell_count, 1)
    cot_flat = state_cot.reshape(cell_count, col_width)
    _, inner, state_full = physics_forward(column, column_in, column_out)
    state_home = jnp.where(ocean_col > 0, state_full, 0.0).astype(jnp.bfloat16)
    target = jnp.where(ocean_col > 0, cot_flat, jnp.zeros_like(cot_flat))
    column_grad, grad_cin, grad_cout = physics_backward(
        column, inner, target, column_in, column_out
    )
    feature_back = jnp.dot(column_grad, decode_weight.T, preferred_element_type=jnp.float32)
    feature_grad = feature_back.astype(jnp.bfloat16)
    hidden_back = jnp.dot(feature_grad, reduce_weight.T, preferred_element_type=jnp.float32)
    expand_grad = gelu_back(expand_pre, hidden_back).astype(jnp.bfloat16)
    normed_back = jnp.dot(expand_grad, expand_weight.T, preferred_element_type=jnp.float32)
    conv_grad = (
        inverse_scale
        * (
            normed_back
            - jnp.mean(normed_back, axis=1, keepdims=True)
            - unit_rows * jnp.mean(normed_back * unit_rows, axis=1, keepdims=True)
        )
    ).astype(jnp.bfloat16)
    grad_decode = jnp.dot(feature.T, column_grad, preferred_element_type=jnp.float32)
    column_sums = shares_sum(
        (grad_cout, grad_cin, grad_decode), device_count, grad_scale
    )
    column_sums, conv_grad = lax.optimization_barrier((column_sums, conv_grad))
    conv_tile = conv_grad.reshape(tile_rows, tile_cols, channels)
    wide_grad = rim_field(conv_tile)
    grad_kernel = kernel_terms(wide_field, conv_tile.astype(jnp.float32), depth_kernel.shape[0])
    grad_expand = jnp.dot(expand_grad.T, normed, preferred_element_type=jnp.float32)
    grad_reduce = jnp.dot(hidden.T, feature_grad, preferred_element_type=jnp.float32)
    kernel_size = depth_kernel.shape[0]
    kernel_rows = jnp.moveaxis(
        grad_kernel.reshape(kernel_size, kernel_size, device_count, channels // device_count), 2, 0
    ).reshape(device_count, 1, -1)
    kernel_rows = jnp.pad(kernel_rows, ((0, 0), (0, 0), (0, channels - kernel_rows.shape[2])))
    mlp_rows, wide_grad = lax.optimization_barrier(
        ((grad_reduce, grad_expand, kernel_rows), wide_grad)
    )
    mlp_sums = shares_sum(mlp_rows, device_count, grad_scale)
    back_terms = back_conv(wide_grad, depth_kernel, tile_rows, tile_cols)
    grad_latent = (
        ocean_mask.astype(jnp.float32)[:, :, None]
        * (feature_back.reshape(tile_rows, tile_cols, channels) + back_terms)
    ).astype(jnp.bfloat16)
    kernel_share = channels // device_count
    state_out = state_home.reshape(tile_rows, tile_cols, col_width)
    return (
        state_out,
        grad_latent,
        mlp_sums[2][0, : kernel_size * kernel_size * kernel_share].reshape(
            kernel_size, kernel_size, kernel_share
        ),
        mlp_sums[1].T,
        mlp_sums[0],
        column_sums[2],
        column_sums[1].T,
        column_sums[0],
    )


def shares_sum(grads, device_count, grad_scale):
    rows = [grad.reshape(device_count, -1, grad.shape[-1]) for grad in grads]
    sizes = [row.shape[1] for row in rows]
    packed = jnp.concatenate(rows, axis=1)
    cores = lax.axis_size("core")
    by_core = packed.reshape((-1, cores, device_count // (lax.axis_size("y") * cores)) + packed.shape[1:])
    core_index = lax.axis_index("core")
    first = core_index == 0
    kept = jnp.where(first, by_core[:, 0], by_core[:, 1])
    given = jnp.where(first, by_core[:, 1], by_core[:, 0])
    pairs = [(i, (i + 1) % cores) for i in range(cores)]
    chip_sum = kept + lax.ppermute(given, "core", pairs)
    chip_sum = chip_sum.reshape((-1,) + packed.shape[1:])
    received = lax.all_to_all(chip_sum, ("y", "lon"), 0, 0, tiled=True)
    total = jnp.sum(received, axis=0) * grad_scale
    outs = []
    offset = 0
    for size in sizes:
        outs.append(total[offset : offset + size])
        offset += size
    return tuple(outs)


def solution(mesh):
    lat_size, lon_size = mesh.devices.shape
    cores = 2
    chip_mesh = Mesh(
        mesh.devices.reshape(lat_size // cores, cores, lon_size), ("y", "core", "lon")
    )
    cells = P(LAT, "lon", None)
    every = (LAT[0], LAT[1], "lon")
    in_specs = (
        cells,
        P(LAT, "lon"),
        P(),
        P(),
        P(),
        P(),
        P(),
        P(),
        cells,
    )
    out_specs = (
        cells,
        cells,
        P(None, None, every),
        P(None, every),
        P(every, None),
        P(every, None),
        P(None, every),
        P(every, None),
    )
    return jax.shard_map(
        local, mesh=chip_mesh, in_specs=in_specs, out_specs=out_specs, check_vma=False
    )
```

```python
import math

import jax
import jax.numpy as jnp
from jax import lax
from jax.sharding import Mesh
from jax.sharding import PartitionSpec as P

KERNEL = 7
LAT = ("y", "core")


EPSILON = 1e-06


def extended(cells, sides, width):
    for axis, dim in sides:
        count = lax.axis_size(axis)
        head = lax.slice_in_dim(cells, 0, width, axis=dim)
        tail = lax.slice_in_dim(cells, cells.shape[dim] - width, cells.shape[dim], axis=dim)
        cells = jnp.concatenate(
            [
                lax.ppermute(tail, axis, [(i, (i + 1) % count) for i in range(count)]),
                cells,
                lax.ppermute(head, axis, [((i + 1) % count, i) for i in range(count)]),
            ],
            axis=dim,
        )
    return cells


def gelu_fn(values_in):
    return jax.nn.gelu(values_in, approximate=True)


def gelu_back(pre_act, upstream):
    return jax.vjp(gelu_fn, pre_act)[1](upstream)[0]


def rim_field(tile_field):
    radius_cells = KERNEL // 2
    widened = extended(tile_field, ((LAT, 0), ("lon", 1)), radius_cells)
    lat_index = lax.axis_index(LAT)
    lat_bands = lax.axis_size(LAT)
    row_ids = jnp.arange(widened.shape[0])
    north_ok = jnp.logical_or(row_ids >= radius_cells, lat_index > 0)
    south_ok = jnp.logical_or(row_ids < widened.shape[0] - radius_cells, lat_index < lat_bands - 1)
    keep_rows = jnp.logical_and(north_ok, south_ok)
    return jnp.where(keep_rows[:, None, None], widened, jnp.zeros_like(widened))


def depthwise(padded, kernel, row_count, col_count):
    summed = jnp.zeros((row_count, col_count, padded.shape[2]), jnp.float32)
    for row_off in range(kernel.shape[0]):
        for col_off in range(kernel.shape[1]):
            window = padded[row_off : row_off + row_count, col_off : col_off + col_count].astype(
                jnp.float32
            )
            summed = summed + kernel[row_off, col_off].astype(jnp.float32) * window
    return summed


def back_conv(wide_grad, kernel, row_count, col_count):
    kernel_span = kernel.shape[0] - 1
    summed = jnp.zeros((row_count, col_count, wide_grad.shape[2]), jnp.float32)
    for row_off in range(kernel.shape[0]):
        for col_off in range(kernel.shape[1]):
            low_row = kernel_span - row_off
            low_col = kernel_span - col_off
            window = wide_grad[low_row : low_row + row_count, low_col : low_col + col_count].astype(
                jnp.float32
            )
            summed = summed + kernel[row_off, col_off].astype(jnp.float32) * window
    return summed


def kernel_terms(wide_field, grad_field, kernel_size):
    row_count = grad_field.shape[0]
    col_count = grad_field.shape[1]
    terms_list = []
    for row_off in range(kernel_size):
        for col_off in range(kernel_size):
            window = wide_field[
                row_off : row_off + row_count, col_off : col_off + col_count
            ].astype(jnp.float32)
            terms_list.append(jnp.sum(grad_field * window, axis=(0, 1)))
    return jnp.stack(terms_list).reshape(kernel_size, kernel_size, grad_field.shape[2])


def physics_forward(col_rows, column_in, column_out):
    column_pre = jnp.dot(col_rows, column_in, preferred_element_type=jnp.float32)
    inner = lax.optimization_barrier(gelu_fn(column_pre).astype(jnp.bfloat16))
    state_full = col_rows.astype(jnp.float32) + jnp.dot(
        inner, column_out, preferred_element_type=jnp.float32
    )
    return (column_pre, inner, state_full)


def physics_backward(col_rows, inner, target, column_in, column_out):
    inner_back = jnp.dot(target, column_out.T, preferred_element_type=jnp.float32)
    again_rows, again_in = lax.optimization_barrier((col_rows, column_in))
    column_pre = jnp.dot(again_rows, again_in, preferred_element_type=jnp.float32)
    column_pre_grad = gelu_back(column_pre, inner_back).astype(jnp.bfloat16)
    column_grad = (
        target.astype(jnp.float32)
        + jnp.dot(column_pre_grad, column_in.T, preferred_element_type=jnp.float32)
    ).astype(jnp.bfloat16)
    grad_cin = jnp.dot(column_pre_grad.T, col_rows, preferred_element_type=jnp.float32)
    rows_t, in_t = lax.optimization_barrier((col_rows, column_in))
    inner_t = gelu_fn(
        jnp.dot(in_t.T, rows_t.T, preferred_element_type=jnp.float32)
    ).astype(jnp.bfloat16)
    grad_cout = jnp.dot(inner_t, target, preferred_element_type=jnp.float32)
    return (column_grad, grad_cin, grad_cout)


def local(
    latent,
    ocean_mask,
    depth_kernel,
    expand_weight,
    reduce_weight,
    decode_weight,
    column_in,
    column_out,
    state_cot,
):
    tile_rows, tile_cols, channels = latent.shape
    cell_count = tile_rows * tile_cols
    col_width = state_cot.shape[2]
    device_count = lax.axis_size(LAT) * lax.axis_size("lon")
    grad_scale = 1.0 / math.sqrt(cell_count * device_count)
    ocean = ocean_mask.astype(latent.dtype)
    masked = latent * ocean[:, :, None]
    wide_field = rim_field(masked)
    convolved = depthwise(wide_field, depth_kernel, tile_rows, tile_cols).reshape(
        cell_count, channels
    )
    row_mean = jnp.mean(convolved, axis=1, keepdims=True)
    centred = convolved - row_mean
    inverse_scale = lax.rsqrt(jnp.mean(centred * centred, axis=1, keepdims=True) + EPSILON)
    unit_rows = centred * inverse_scale
    normed = unit_rows.astype(jnp.bfloat16)
    expand_pre = jnp.dot(normed, expand_weight, preferred_element_type=jnp.float32)
    hidden = gelu_fn(expand_pre).astype(jnp.bfloat16)
    masked_flat = masked.reshape(cell_count, channels)
    feature = (
        masked_flat.astype(jnp.float32)
        + jnp.dot(hidden, reduce_weight, preferred_element_type=jnp.float32)
    ).astype(jnp.bfloat16)
    column = jnp.dot(feature, decode_weight, preferred_element_type=jnp.float32).astype(
        jnp.bfloat16
    )
    ocean_col = ocean_mask.reshape(cell_count, 1)
    cot_flat = state_cot.reshape(cell_count, col_width)
    _, inner, state_full = physics_forward(column, column_in, column_out)
    state_home = jnp.where(ocean_col > 0, state_full, 0.0).astype(jnp.bfloat16)
    target = jnp.where(ocean_col > 0, cot_flat, jnp.zeros_like(cot_flat))
    column_grad, grad_cin, grad_cout = physics_backward(
        column, inner, target, column_in, column_out
    )
    feature_back = jnp.dot(column_grad, decode_weight.T, preferred_element_type=jnp.float32)
    feature_grad = feature_back.astype(jnp.bfloat16)
    hidden_back = jnp.dot(feature_grad, reduce_weight.T, preferred_element_type=jnp.float32)
    expand_grad = gelu_back(expand_pre, hidden_back).astype(jnp.bfloat16)
    normed_back = jnp.dot(expand_grad, expand_weight.T, preferred_element_type=jnp.float32)
    conv_grad = (
        inverse_scale
        * (
            normed_back
            - jnp.mean(normed_back, axis=1, keepdims=True)
            - unit_rows * jnp.mean(normed_back * unit_rows, axis=1, keepdims=True)
        )
    ).astype(jnp.bfloat16)
    grad_decode = jnp.dot(feature.T, column_grad, preferred_element_type=jnp.float32)
    column_sums = shares_sum(
        (grad_cout, grad_cin, grad_decode), device_count, grad_scale
    )
    column_sums, conv_grad = lax.optimization_barrier((column_sums, conv_grad))
    conv_tile = conv_grad.reshape(tile_rows, tile_cols, channels)
    wide_grad = rim_field(conv_tile)
    grad_kernel = kernel_terms(wide_field, conv_tile.astype(jnp.float32), depth_kernel.shape[0])
    grad_expand = jnp.dot(expand_grad.T, normed, preferred_element_type=jnp.float32)
    grad_reduce = jnp.dot(hidden.T, feature_grad, preferred_element_type=jnp.float32)
    kernel_size = depth_kernel.shape[0]
    kernel_rows = jnp.moveaxis(
        grad_kernel.reshape(kernel_size, kernel_size, device_count, channels // device_count), 2, 0
    ).reshape(device_count, 1, -1)
    kernel_rows = jnp.pad(kernel_rows, ((0, 0), (0, 0), (0, channels - kernel_rows.shape[2])))
    mlp_rows, wide_grad = lax.optimization_barrier(
        ((grad_reduce, grad_expand, kernel_rows), wide_grad)
    )
    mlp_sums = shares_sum(mlp_rows, device_count, grad_scale)
    back_terms = back_conv(wide_grad, depth_kernel, tile_rows, tile_cols)
    grad_latent = (
        ocean_mask.astype(jnp.float32)[:, :, None]
        * (feature_back.reshape(tile_rows, tile_cols, channels) + back_terms)
    ).astype(jnp.bfloat16)
    kernel_share = channels // device_count
    state_out = state_home.reshape(tile_rows, tile_cols, col_width)
    return (
        state_out,
        grad_latent,
        mlp_sums[2][0, : kernel_size * kernel_size * kernel_share].reshape(
            kernel_size, kernel_size, kernel_share
        ),
        mlp_sums[1].T,
        mlp_sums[0],
        column_sums[2],
        column_sums[1].T,
        column_sums[0],
    )


def shares_sum(grads, device_count, grad_scale):
    rows = [grad.reshape(device_count, -1, grad.shape[-1]) for grad in grads]
    sizes = [row.shape[1] for row in rows]
    packed = jnp.concatenate(rows, axis=1)
    cores = lax.axis_size("core")
    by_core = packed.reshape((-1, cores, device_count // (lax.axis_size("y") * cores)) + packed.shape[1:])
    core_index = lax.axis_index("core")
    first = core_index == 0
    kept = jnp.where(first, by_core[:, 0], by_core[:, 1])
    given = jnp.where(first, by_core[:, 1], by_core[:, 0])
    pairs = [(i, (i + 1) % cores) for i in range(cores)]
    chip_sum = kept + lax.ppermute(given, "core", pairs)
    chip_sum = chip_sum.reshape((-1,) + packed.shape[1:])
    received = lax.all_to_all(chip_sum, ("y", "lon"), 0, 0, tiled=True)
    total = jnp.sum(received, axis=0) * grad_scale
    outs = []
    offset = 0
    for size in sizes:
        outs.append(total[offset : offset + size])
        offset += size
    return tuple(outs)


def solution(mesh):
    lat_size, lon_size = mesh.devices.shape
    cores = 2
    chip_mesh = Mesh(
        mesh.devices.reshape(lat_size // cores, cores, lon_size), ("y", "core", "lon")
    )
    cells = P(LAT, "lon", None)
    every = (LAT[0], LAT[1], "lon")
    in_specs = (
        cells,
        P(LAT, "lon"),
        P(),
        P(),
        P(),
        P(),
        P(),
        P(),
        cells,
    )
    out_specs = (
        cells,
        cells,
        P(None, None, every),
        P(None, every),
        P(every, None),
        P(every, None),
        P(None, every),
        P(every, None),
    )
    return jax.shard_map(
        local, mesh=chip_mesh, in_specs=in_specs, out_specs=out_specs, check_vma=False
    )
```
